512 devices in a mesh: tm: 32 (over x, z_lo, core), height: 4 (over y), width: 4 (over z_hi).
Axes of the slice: x: 4, y: 4, z: 16 (z_hi: 4, z_lo: 4; z = z_hi * 4 + z_lo), core: 2. Of those that a mesh axis runs over, the one named last changes fastest.
Arguments:
- queries: bfloat16 [4, 4, 1024, 512], P('height', 'width'), may hold values from -40 to 40
- kv_blocks: bfloat16 [2, 64, 4, 4, 2, 64, 512], P(None, 'tm', 'height', 'width'), may hold values from -8 to 8
- block_list: int32 [4, 4, 8], P('height', 'width'), may hold values from 0 to 17, as said below
- block_valid: int32 [4, 4, 8], P('height', 'width'), may hold values from 0 to 1, as said below
- w_out: bfloat16 [512, 512], replicated, may hold values from -0.25 to 0.25
Outputs:
- joined: float32 [4, 4, 1024, 512], P('height', 'width', 'tm')
The draws below stay inside these ranges and needn't reach their ends.
Inputs may be any that keep to these rules, and one draw needn't show every extreme that they name: `block_list`: the entries of one tile are distinct and each names a block of a tile inside the image. `block_valid`: in each tile the used entries come first, 4 to 8 of them.
All inputs are finite; a program needn't handle non-finite values.
Results may differ from the reference program's by a relative error of at most 0.0039.
Values may be sent and summed in bfloat16 or wider, within the bound.
No kernel may reach another device: no remote copies, remote signals or barrier semaphores. Data moves between devices by JAX's collectives and lax.ppermute only.
A program may use at most 192 MiB of HBM per device.

```python
import jax
import jax.numpy as jnp
from jax import lax

D = 512
HEADS = 8
HD = 64
QT = 1024
F_DEV = 2
BLK = 64
NBLK = 2
NLIST = 8
FRAMES = 64
TILE_ROWS = 4
TILE_COLS = 4
N_TM = 32


def draw_queries(key, part):
    shape = (TILE_ROWS, TILE_COLS, QT, D)
    first = jax.random.fold_in(key, 1)
    result = jnp.clip(jax.random.normal(first, shape, jnp.float32), -6.0, 6.0)
    return result.astype(jnp.bfloat16)


def draw_kv_blocks(key, part):
    shape = (2, FRAMES, TILE_ROWS, TILE_COLS, NBLK, BLK, D)
    second = jax.random.fold_in(key, 2)
    result = jnp.clip(jax.random.normal(second, shape, jnp.float32), -6.0, 6.0)
    return result.astype(jnp.bfloat16)


def draw_block_list(key, part):
    cands = 9 * NBLK
    raw = jax.random.randint(key, (TILE_ROWS, TILE_COLS, cands), 0, 1 << 20)
    order = jnp.arange(cands, dtype=jnp.int32)
    scored = raw * cands + order
    row_off = order // (3 * NBLK) - 1
    col_off = order // NBLK % 3 - 1
    rows = jnp.arange(TILE_ROWS, dtype=jnp.int32)[:, None, None] + row_off[None, None, :]
    cols = jnp.arange(TILE_COLS, dtype=jnp.int32)[None, :, None] + col_off[None, None, :]
    inside = (rows >= 0) & (rows < TILE_ROWS) & (cols >= 0) & (cols < TILE_COLS)
    scored = jnp.where(inside, scored, -1 - order)
    scored = scored.at[0, 0, cands - 1].set(1 << 30)
    scored = scored.at[TILE_ROWS - 1, TILE_COLS - 1, 0].set(1 << 30)
    ranked = jnp.argsort(-scored, axis=-1)
    return ranked[:, :, :NLIST].astype(jnp.int32)


def draw_block_valid(key, part):
    counts = jax.random.randint(jax.random.fold_in(key, 6), (TILE_ROWS, TILE_COLS, 1), NLIST // 2, NLIST + 1)
    counts = counts.at[0, 0, 0].set(NLIST)
    counts = counts.at[TILE_ROWS - 1, TILE_COLS - 1, 0].set(NLIST // 2)
    slots = jnp.arange(NLIST, dtype=jnp.int32)[None, None, :]
    return (slots < counts).astype(jnp.int32)


def normal_values(rng, extent, scale, bound, held_as=jnp.bfloat16):
    return jnp.clip(scale * jax.random.normal(rng, extent, jnp.float32), -bound, bound).astype(held_as)


def setup_inputs(seed: int = 0) -> dict:
    key_of = jax.random.split(jax.random.key(seed), 6)
    queries = draw_queries(jax.random.fold_in(key_of[5], 71), 0)
    kv_blocks = draw_kv_blocks(jax.random.fold_in(key_of[5], 71), 0)
    block_list = draw_block_list(jax.random.fold_in(key_of[5], 71), 0)
    block_valid = draw_block_valid(jax.random.fold_in(key_of[5], 71), 0)
    w_out = normal_values(key_of[4], (D, D), D ** -0.5, 0.25)
    return {"queries": queries, "kv_blocks": kv_blocks, "block_list": block_list, "block_valid": block_valid, "w_out": w_out}


def group_partial(query_rows, keys, values, keep):
    count = query_rows.shape[0]
    query_heads = query_rows.reshape(count, HEADS, HD).astype(jnp.float32)
    key_heads = keys.reshape(-1, HEADS, HD).astype(jnp.float32)
    value_heads = values.reshape(-1, HEADS, HD).astype(jnp.float32)
    scores = jnp.einsum('qhd,khd->hqk', query_heads, key_heads) / jnp.sqrt(jnp.float32(HD))
    scores = jnp.where(keep[None, None, :], scores, jnp.float32(-1e+30))
    row_top = lax.optimization_barrier(jnp.max(scores, axis=2))
    probs = jnp.where(keep[None, None, :], jnp.exp(scores - row_top[:, :, None]), jnp.float32(0.0))
    totals = lax.optimization_barrier(jnp.sum(probs, axis=2))
    probs = probs.astype(jnp.bfloat16).astype(jnp.float32)
    outputs = jnp.einsum('hqk,khd->qhd', probs, value_heads).reshape(count, D)
    return (row_top.T, totals.T, outputs)

def reference(queries, kv_blocks, block_list, block_valid, w_out):
    padded = jnp.pad(kv_blocks, ((0, 0), (0, 0), (1, 1), (1, 1), (0, 0), (0, 0), (0, 0)))

    def one_tile(flat):
        row = flat // TILE_COLS
        col = flat % TILE_COLS
        zero = jnp.zeros((), jnp.int32)
        hood = lax.dynamic_slice(padded, (zero, zero, row, col, zero, zero, zero), (2, FRAMES, 3, 3, NBLK, BLK, D))
        hood = hood.reshape(2, FRAMES, 9 * NBLK, BLK, D)
        listed = block_list[row, col]
        chosen = jnp.take(hood, listed, axis=2)
        keep_list = block_valid[row, col] > 0
        keep = jnp.broadcast_to(keep_list[None, :, None], (F_DEV, NLIST, BLK)).reshape(-1)
        query_rows = queries[row, col]
        grouped = chosen.reshape(2, N_TM, F_DEV * NLIST * BLK, D)

        def one_group(group):
            return group_partial(query_rows, grouped[0, group], grouped[1, group], keep)
        tops, totals, outputs = lax.map(one_group, jnp.arange(N_TM, dtype=jnp.int32))
        overall = lax.optimization_barrier(jnp.max(tops, axis=0))
        factor = jnp.exp(tops - overall[None])
        total = lax.optimization_barrier(jnp.sum(totals * factor, axis=0))
        summed = lax.optimization_barrier(jnp.sum(outputs * jnp.repeat(factor, HD, axis=2), axis=0))
        attended = summed / jnp.repeat(total, HD, axis=1)
        normed = attended * lax.rsqrt(lax.optimization_barrier(jnp.mean(attended * attended, axis=1, keepdims=True)) + 1e-06)
        normed = normed.astype(jnp.bfloat16)
        return jnp.dot(normed, w_out, preferred_element_type=jnp.float32)
    tiles = lax.map(one_tile, jnp.arange(TILE_ROWS * TILE_COLS, dtype=jnp.int32))
    return tiles.reshape(TILE_ROWS, TILE_COLS, QT, D)
```

```python
import jax
import jax.numpy as jnp
from jax import lax
from jax.sharding import PartitionSpec as P

HEADS = 8
HD = 64


def shifted(array, axis, forward):
    size = lax.axis_size(axis)
    if forward:
        pairs = [(i, i + 1) for i in range(size - 1)]
    else:
        pairs = [(i + 1, i) for i in range(size - 1)]
    return lax.ppermute(array, axis, pairs)


def neighbourhood(kv_blocks):
    left = shifted(kv_blocks, "width", True)
    right = shifted(kv_blocks, "width", False)
    row = jnp.concatenate([left, kv_blocks, right], axis=3)
    up = shifted(row, "height", True)
    down = shifted(row, "height", False)
    return jnp.concatenate([up, row, down], axis=2)


def group_partial(query_rows, keys, values, keep):
    count = query_rows.shape[0]
    query_heads = query_rows.reshape(count, HEADS, HD)
    key_heads = keys.reshape(-1, HEADS, HD)
    value_heads = values.reshape(-1, HEADS, HD)
    scores = jnp.einsum("qhd,khd->hqk", query_heads, key_heads, preferred_element_type=jnp.float32)
    scores = scores / jnp.sqrt(jnp.float32(HD))
    scores = jnp.where(keep[None, None, :], scores, jnp.float32(-1e30))
    row_top = jnp.max(scores, axis=2)
    probs = jnp.where(keep[None, None, :], jnp.exp(scores - row_top[:, :, None]), jnp.float32(0.0))
    totals = jnp.sum(probs, axis=2)
    outputs = jnp.einsum(
        "hqk,khd->qhd", probs.astype(jnp.bfloat16), value_heads, preferred_element_type=jnp.float32
    )
    return (row_top.T, totals.T, outputs.reshape(count, HEADS * HD))


def merge(stats_a, out_a, stats_b, out_b):
    heads = stats_a.shape[-1] // 2
    top_a, tot_a = stats_a[..., :heads], stats_a[..., heads:]
    top_b, tot_b = stats_b[..., :heads], stats_b[..., heads:]
    top = jnp.maximum(top_a, top_b)
    fa = jnp.exp(top_a - top)
    fb = jnp.exp(top_b - top)
    tot = tot_a * fa + tot_b * fb
    shape = out_a.shape
    out = (
        out_a.reshape(shape[:-1] + (heads, -1)) * fa[..., None]
        + out_b.reshape(shape[:-1] + (heads, -1)) * fb[..., None]
    ).reshape(shape)
    return jnp.concatenate([top, tot], axis=-1), out


def tree_reduce(stats, out):
    groups = lax.axis_size("tm")
    nbits = groups.bit_length() - 1
    me = lax.axis_index("tm")
    rows = out.shape[0]
    blk = rows // groups
    stats = stats.reshape((2,) * nbits + (blk, stats.shape[-1]))
    out = out.reshape((2,) * nbits + (blk, out.shape[-1]))
    order = [0, 1, 3, 2, 4] if nbits == 5 else list(range(nbits))
    remaining = list(range(nbits - 1, -1, -1))
    for bit in order:
        axis = remaining.index(bit)
        remaining.remove(bit)
        mine = (me >> bit) & 1
        pairs = [(t, t ^ (1 << bit)) for t in range(groups)]
        keep_s = lax.dynamic_index_in_dim(stats, mine, axis, keepdims=False)
        keep_o = lax.dynamic_index_in_dim(out, mine, axis, keepdims=False)
        send_s = lax.dynamic_index_in_dim(stats, 1 - mine, axis, keepdims=False)
        send_o = lax.dynamic_index_in_dim(out, 1 - mine, axis, keepdims=False)
        got_s = lax.ppermute(send_s, "tm", pairs)
        got_o = lax.ppermute(send_o, "tm", pairs)
        stats, out = merge(keep_s, keep_o, got_s, got_o)
    return stats.reshape(blk, -1), out.reshape(blk, -1)


def local(queries, kv_blocks, block_list, block_valid, w_out):
    hood = neighbourhood(kv_blocks)
    frames = hood.shape[1]
    nblk = hood.shape[4]
    blk = hood.shape[5]
    width = hood.shape[6]
    hood = hood.reshape(2, frames, 9 * nblk, blk, width)
    listed = block_list[0, 0]
    nlist = listed.shape[0]
    chosen = jnp.take(hood, listed, axis=2)
    keep = jnp.broadcast_to((block_valid[0, 0] > 0)[None, :, None], (frames, nlist, blk)).reshape(
        -1
    )
    keys = chosen[0].reshape(-1, width)
    values = chosen[1].reshape(-1, width)
    query_rows = queries[0, 0]
    qtok = query_rows.shape[0]
    step_rows = min(512, qtok)

    def one_block(rows):
        return group_partial(rows, keys, values, keep)

    tops, totals, outputs = lax.map(
        one_block, query_rows.reshape(qtok // step_rows, step_rows, width)
    )
    tops = tops.reshape(qtok, HEADS)
    totals = totals.reshape(qtok, HEADS)
    outputs = outputs.reshape(qtok, width)
    stats = jnp.concatenate([tops, totals], axis=-1)
    stats, summed = tree_reduce(stats, outputs)
    total = stats[:, HEADS:]
    own_rows = summed.shape[0]
    attended = summed / jnp.repeat(total, HD, axis=1)
    normed = attended * lax.rsqrt(jnp.mean(attended * attended, axis=1, keepdims=True) + 1e-06)
    normed = normed.astype(jnp.bfloat16)
    joined = jnp.dot(normed, w_out, preferred_element_type=jnp.float32)
    return joined.reshape(1, 1, own_rows, width)


def solution(mesh):
    in_specs = (
        P("height", "width", None, None),
        P(None, "tm", "height", "width", None, None, None),
        P("height", "width", None),
        P("height", "width", None),
        P(),
    )
    out_specs = P("height", "width", "tm", None)
    return jax.shard_map(local, mesh=mesh, in_specs=in_specs, out_specs=out_specs, check_vma=False)
```

```python
import functools

import jax
import jax.numpy as jnp
from jax import lax
from jax.sharding import PartitionSpec as P

HEADS = 8
HD = 64


def shifted(array, axis, forward):
    size = lax.axis_size(axis)
    if forward:
        pairs = [(i, i + 1) for i in range(size - 1)]
    else:
        pairs = [(i + 1, i) for i in range(size - 1)]
    return lax.ppermute(array, axis, pairs)


def neighbourhood(kv_blocks):
    left = shifted(kv_blocks, "width", True)
    right = shifted(kv_blocks, "width", False)
    up_mid = shifted(kv_blocks, "height", True)
    down_mid = shifted(kv_blocks, "height", False)
    sides = jnp.concatenate([left, right], axis=3)
    up_sides = shifted(sides, "height", True)
    down_sides = shifted(sides, "height", False)
    row = jnp.concatenate([left, kv_blocks, right], axis=3)
    up = jnp.concatenate([up_sides[:, :, :, :1], up_mid, up_sides[:, :, :, 1:]], axis=3)
    down = jnp.concatenate([down_sides[:, :, :, :1], down_mid, down_sides[:, :, :, 1:]], axis=3)
    return jnp.concatenate([up, row, down], axis=2)


def attend(q, kv, keep, count):
    heads, qtok, hd = q.shape
    halves = q.reshape(heads, 2, qtok // 2, hd).transpose(1, 0, 2, 3)
    stats, out = lax.map(lambda part: attend_rows(part, kv, keep, count), halves)
    stats = stats.transpose(1, 2, 0, 3).reshape(2, heads, qtok)
    out = out.transpose(1, 0, 2, 3).reshape(heads, qtok, hd)
    return stats, out


def attend_rows(q, kv, keep, count):
    keys = kv[0, :, :count]
    values = kv[1, :, :count]
    keep = keep[:count]
    scores = jnp.einsum("hqd,hkd->hqk", q, keys, preferred_element_type=jnp.float32)
    scores = scores / jnp.sqrt(jnp.float32(HD))
    scores = jnp.where(keep[None, None, :], scores, jnp.float32(-1e30))
    top = jnp.max(scores, axis=2)
    probs = jnp.where(keep[None, None, :], jnp.exp(scores - top[:, :, None]), jnp.float32(0.0))
    total = jnp.sum(probs, axis=2)
    out = jnp.einsum(
        "hqk,hkd->hqd", probs.astype(jnp.bfloat16), values, preferred_element_type=jnp.float32
    )
    return jnp.stack([top, total]), out


def merge(stats_a, out_a, stats_b, out_b):
    top = jnp.maximum(stats_a[0], stats_b[0])
    fa = jnp.exp(stats_a[0] - top)
    fb = jnp.exp(stats_b[0] - top)
    tot = stats_a[1] * fa + stats_b[1] * fb
    out = out_a * fa[..., None] + out_b * fb[..., None]
    return jnp.stack([top, tot]), out


def tree_reduce(stats, out):
    groups = lax.axis_size("tm")
    nbits = groups.bit_length() - 1
    me = lax.axis_index("tm")
    rows = out.shape[1]
    blk = rows // groups
    heads = out.shape[0]
    stats = stats.reshape((2, heads) + (2,) * nbits + (blk,))
    out = out.reshape((heads,) + (2,) * nbits + (blk, out.shape[-1]))
    order = [0, 1, 3, 2, 4] if nbits == 5 else list(range(nbits))
    remaining = list(range(nbits - 1, -1, -1))
    for bit in order:
        axis = remaining.index(bit)
        remaining.remove(bit)
        mine = (me >> bit) & 1
        pairs = [(t, t ^ (1 << bit)) for t in range(groups)]
        keep_s = lax.dynamic_index_in_dim(stats, mine, axis + 2, keepdims=False)
        keep_o = lax.dynamic_index_in_dim(out, mine, axis + 1, keepdims=False)
        send_s = lax.dynamic_index_in_dim(stats, 1 - mine, axis + 2, keepdims=False)
        send_o = lax.dynamic_index_in_dim(out, 1 - mine, axis + 1, keepdims=False)
        got_s = lax.ppermute(send_s, "tm", pairs)
        got_o = lax.ppermute(send_o, "tm", pairs)
        stats, out = merge(keep_s, keep_o, got_s, got_o)
    return stats, out


def local(queries, kv_blocks, block_list, block_valid, w_out):
    hood = neighbourhood(kv_blocks)
    frames = hood.shape[1]
    nblk = hood.shape[4]
    blk = hood.shape[5]
    width = hood.shape[6]
    hood = hood.reshape(2, frames, 9 * nblk, blk, width)
    listed = block_list[0, 0]
    nlist = listed.shape[0]
    chosen = jnp.take(hood, listed, axis=2)
    kv = chosen.transpose(0, 2, 1, 3, 4).reshape(2, nlist * frames * blk, HEADS, HD)
    kv = kv.transpose(0, 2, 1, 3)
    query_rows = queries[0, 0]
    qtok = query_rows.shape[0]
    q = query_rows.reshape(qtok, HEADS, HD).transpose(1, 0, 2)
    valid = block_valid[0, 0] > 0
    used = jnp.sum(valid.astype(jnp.int32))
    keep = jnp.broadcast_to(valid[:, None], (nlist, frames * blk)).reshape(-1)
    least = nlist // 2
    branches = [
        functools.partial(attend, count=c * frames * blk) for c in range(least, nlist + 1, 2)
    ]
    stats, out = lax.switch((used - least + 1) // 2, branches, q, kv, keep)
    stats, summed = tree_reduce(stats, out)
    total = stats[1]
    attended = summed / total[..., None]
    own_rows = attended.shape[1]
    attended = attended.transpose(1, 0, 2).reshape(own_rows, width)
    normed = attended * lax.rsqrt(jnp.mean(attended * attended, axis=1, keepdims=True) + 1e-06)
    normed = normed.astype(jnp.bfloat16)
    joined = jnp.dot(normed, w_out, preferred_element_type=jnp.float32)
    return joined.reshape(1, 1, own_rows, width)


def solution(mesh):
    in_specs = (
        P("height", "width", None, None),
        P(None, "tm", "height", "width", None, None, None),
        P("height", "width", None),
        P("height", "width", None),
        P(),
    )
    out_specs = P("height", "width", "tm", None)
    return jax.shard_map(local, mesh=mesh, in_specs=in_specs, out_specs=out_specs, check_vma=False)
```

```python
import jax
import jax.numpy as jnp
from jax import lax
from jax.experimental import pallas as pl
from jax.experimental.pallas import tpu as pltpu
from jax.sharding import PartitionSpec as P

HEADS = 8
HD = 64
TQ = 256


def shifted(array, axis, forward):
    size = lax.axis_size(axis)
    if forward:
        pairs = [(i, i + 1) for i in range(size - 1)]
    else:
        pairs = [(i + 1, i) for i in range(size - 1)]
    return lax.ppermute(array, axis, pairs)


def neighbourhood(kv_blocks):
    left = shifted(kv_blocks, "width", True)
    right = shifted(kv_blocks, "width", False)
    up_mid = shifted(kv_blocks, "height", True)
    down_mid = shifted(kv_blocks, "height", False)
    left, right, up_mid, down_mid = lax.optimization_barrier((left, right, up_mid, down_mid))
    sides = jnp.concatenate([left, right], axis=3)
    up_sides = shifted(sides, "height", True)
    down_sides = shifted(sides, "height", False)
    row = jnp.concatenate([left, kv_blocks, right], axis=3)
    up = jnp.concatenate([up_sides[:, :, :, :1], up_mid, up_sides[:, :, :, 1:]], axis=3)
    down = jnp.concatenate([down_sides[:, :, :, :1], down_mid, down_sides[:, :, :, 1:]], axis=3)
    return jnp.concatenate([up, row, down], axis=2)


def attention_kernel(q_ref, k_ref, v_ref, keep_ref, o_ref, st_ref):
    rows = q_ref.shape[0]
    keep = keep_ref[...] > 0
    lane = lax.broadcasted_iota(jnp.int32, (1, 2 * HD), 1)
    low = lane < HD
    stat_lane = lax.broadcasted_iota(jnp.int32, (1, 2 * HEADS), 1)
    stats = jnp.zeros((rows, 2 * HEADS), jnp.float32)
    for pair in range(HEADS // 2):
        cols = pl.ds(pair * 2 * HD, 2 * HD)
        q2 = q_ref[:, cols]
        k2 = k_ref[:, cols]
        v2 = v_ref[:, cols]
        outs = []
        for half in range(2):
            mine = low if half == 0 else jnp.logical_not(low)
            qh = jnp.where(mine, q2, jnp.zeros_like(q2))
            scores = lax.dot_general(
                qh, k2, (((1,), (1,)), ((), ())), preferred_element_type=jnp.float32
            )
            scores = scores / jnp.float32(8.0)
            scores = jnp.where(keep, scores, jnp.float32(-1e30))
            top = jnp.max(scores, axis=1, keepdims=True)
            probs = jnp.where(keep, jnp.exp(scores - top), jnp.float32(0.0))
            total = jnp.sum(probs, axis=1, keepdims=True)
            outs.append(
                jnp.dot(probs.astype(jnp.bfloat16), v2, preferred_element_type=jnp.float32)
            )
            head = pair * 2 + half
            stats = jnp.where(stat_lane == head, top, stats)
            stats = jnp.where(stat_lane == HEADS + head, total, stats)
        o_ref[:, cols] = jnp.where(low, outs[0], outs[1])
    st_ref[...] = stats


def attention(query_rows, keys, values, keep):
    qtok, width = query_rows.shape
    count = keys.shape[0]
    flops = 2 * 2 * qtok * count * 2 * width
    return pl.pallas_call(
        attention_kernel,
        grid=(qtok // TQ,),
        in_specs=[
            pl.BlockSpec((TQ, width), lambda i: (i, 0)),
            pl.BlockSpec((count, width), lambda i: (0, 0)),
            pl.BlockSpec((count, width), lambda i: (0, 0)),
            pl.BlockSpec((1, count), lambda i: (0, 0)),
        ],
        out_specs=[
            pl.BlockSpec((TQ, width), lambda i: (i, 0)),
            pl.BlockSpec((TQ, 2 * HEADS), lambda i: (i, 0)),
        ],
        out_shape=[
            jax.ShapeDtypeStruct((qtok, width), jnp.float32),
            jax.ShapeDtypeStruct((qtok, 2 * HEADS), jnp.float32),
        ],
        cost_estimate=pl.CostEstimate(
            flops=flops,
            transcendentals=qtok * count * HEADS,
            bytes_accessed=qtok * width * 6 + count * width * 4,
        ),
    )(query_rows, keys, values, keep)


def merge(stats_a, out_a, stats_b, out_b):
    heads = stats_a.shape[-1] // 2
    top_a, tot_a = stats_a[..., :heads], stats_a[..., heads:]
    top_b, tot_b = stats_b[..., :heads], stats_b[..., heads:]
    top = jnp.maximum(top_a, top_b)
    fa = jnp.exp(top_a - top)
    fb = jnp.exp(top_b - top)
    tot = tot_a * fa + tot_b * fb
    shape = out_a.shape
    out = (
        out_a.reshape(shape[:-1] + (heads, -1)) * fa[..., None]
        + out_b.reshape(shape[:-1] + (heads, -1)) * fb[..., None]
    ).reshape(shape)
    return jnp.concatenate([top, tot], axis=-1), out


def tree_reduce(stats, out):
    groups = lax.axis_size("tm")
    nbits = groups.bit_length() - 1
    me = lax.axis_index("tm")
    rows = out.shape[0]
    blk = rows // groups
    stats = stats.reshape((2,) * nbits + (blk, stats.shape[-1]))
    out = out.reshape((2,) * nbits + (blk, out.shape[-1]))
    order = [0, 1, 3, 2, 4] if nbits == 5 else list(range(nbits))
    remaining = list(range(nbits - 1, -1, -1))
    for bit in order:
        axis = remaining.index(bit)
        remaining.remove(bit)
        mine = (me >> bit) & 1
        pairs = [(t, t ^ (1 << bit)) for t in range(groups)]
        keep_s = lax.dynamic_index_in_dim(stats, mine, axis, keepdims=False)
        keep_o = lax.dynamic_index_in_dim(out, mine, axis, keepdims=False)
        send_s = lax.dynamic_index_in_dim(stats, 1 - mine, axis, keepdims=False)
        send_o = lax.dynamic_index_in_dim(out, 1 - mine, axis, keepdims=False)
        got_s = lax.ppermute(send_s, "tm", pairs)
        got_o = lax.ppermute(send_o, "tm", pairs)
        stats, out = merge(keep_s, keep_o, got_s, got_o)
    return stats.reshape(blk, -1), out.reshape(blk, -1)


def local(queries, kv_blocks, block_list, block_valid, w_out):
    hood = neighbourhood(kv_blocks)
    frames = hood.shape[1]
    nblk = hood.shape[4]
    blk = hood.shape[5]
    width = hood.shape[6]
    hood = hood.reshape(2, frames, 9 * nblk, blk, width)
    listed = block_list[0, 0]
    nlist = listed.shape[0]
    chosen = jnp.take(hood, listed, axis=2)
    keep = jnp.broadcast_to((block_valid[0, 0] > 0)[None, :, None], (frames, nlist, blk))
    keep = keep.reshape(1, -1).astype(jnp.int32)
    keys = chosen[0].reshape(-1, width)
    values = chosen[1].reshape(-1, width)
    query_rows = queries[0, 0]
    outputs, stats = attention(query_rows, keys, values, keep)
    stats, summed = tree_reduce(stats, outputs)
    total = stats[:, HEADS:]
    own_rows = summed.shape[0]
    attended = summed / jnp.repeat(total, HD, axis=1)
    normed = attended * lax.rsqrt(jnp.mean(attended * attended, axis=1, keepdims=True) + 1e-06)
    normed = normed.astype(jnp.bfloat16)
    joined = jnp.dot(normed, w_out, preferred_element_type=jnp.float32)
    return joined.reshape(1, 1, own_rows, width)


def solution(mesh):
    in_specs = (
        P("height", "width", None, None),
        P(None, "tm", "height", "width", None, None, None),
        P("height", "width", None),
        P("height", "width", None),
        P(),
    )
    out_specs = P("height", "width", "tm", None)
    return jax.shard_map(local, mesh=mesh, in_specs=in_specs, out_specs=out_specs, check_vma=False)
```

```python
import jax
import jax.numpy as jnp
from jax import lax
from jax.experimental import pallas as pl
from jax.experimental.pallas import tpu as pltpu
from jax.sharding import PartitionSpec as P

HEADS = 8
HD = 64
TQ = 256


def shifted(array, axis, forward):
    size = lax.axis_size(axis)
    if forward:
        pairs = [(i, i + 1) for i in range(size - 1)]
    else:
        pairs = [(i + 1, i) for i in range(size - 1)]
    return lax.ppermute(array, axis, pairs)


def neighbourhood(kv_blocks):
    up_mid = shifted(kv_blocks, "height", True)
    down_mid = shifted(kv_blocks, "height", False)
    frames = kv_blocks.shape[1]
    rows = []
    for f in range(frames):
        own = kv_blocks[:, f : f + 1]
        left = shifted(own, "width", True)
        right = shifted(own, "width", False)
        sides = jnp.concatenate([left, right], axis=3)
        up_sides = shifted(sides, "height", True)
        down_sides = shifted(sides, "height", False)
        row = jnp.concatenate([left, own, right], axis=3)
        rows.append((row, up_sides, down_sides))
    row = jnp.concatenate([r[0] for r in rows], axis=1)
    up_sides = jnp.concatenate([r[1] for r in rows], axis=1)
    down_sides = jnp.concatenate([r[2] for r in rows], axis=1)
    up = jnp.concatenate([up_sides[:, :, :, :1], up_mid, up_sides[:, :, :, 1:]], axis=3)
    down = jnp.concatenate([down_sides[:, :, :, :1], down_mid, down_sides[:, :, :, 1:]], axis=3)
    return jnp.concatenate([up, row, down], axis=2)


PACK = 128


def attention_kernel(q_ref, k_ref, v_ref, keep_ref, first_ref, second_ref):
    rows = q_ref.shape[0]
    step = pl.program_id(0)
    half = pl.num_programs(0) // 2
    keep = keep_ref[...] > 0
    lane = lax.broadcasted_iota(jnp.int32, (1, 2 * HD), 1)
    low = lane < HD
    stat_lane = lax.broadcasted_iota(jnp.int32, (1, PACK), 1)
    stats = jnp.zeros((rows, PACK), jnp.float32)
    blocks = []
    for pair in range(HEADS // 2):
        cols = pl.ds(pair * 2 * HD, 2 * HD)
        q2 = q_ref[:, cols]
        k2 = k_ref[:, cols]
        v2 = v_ref[:, cols]
        outs = []
        for part in range(2):
            mine = low if part == 0 else jnp.logical_not(low)
            qh = jnp.where(mine, q2, jnp.zeros_like(q2))
            scores = lax.dot_general(
                qh, k2, (((1,), (1,)), ((), ())), preferred_element_type=jnp.float32
            )
            scores = scores / jnp.float32(8.0)
            scores = jnp.where(keep, scores, jnp.float32(-1e30))
            top = jnp.max(scores, axis=1, keepdims=True)
            probs = jnp.where(keep, jnp.exp(scores - top), jnp.float32(0.0))
            total = jnp.sum(probs, axis=1, keepdims=True)
            outs.append(
                jnp.dot(probs.astype(jnp.bfloat16), v2, preferred_element_type=jnp.float32)
            )
            head = pair * 2 + part
            stats = jnp.where(stat_lane == head, top, stats)
            stats = jnp.where(stat_lane == HEADS + head, total, stats)
        blocks.append(jnp.where(low, outs[0], outs[1]))
    packed = jnp.concatenate(blocks + [stats], axis=1)

    @pl.when(step < half)
    def _():
        first_ref[...] = packed

    @pl.when(step >= half)
    def _():
        second_ref[...] = packed


def attention(query_rows, keys, values, keep):
    qtok, width = query_rows.shape
    count = keys.shape[0]
    tiles = qtok // TQ
    half = tiles // 2
    flops = 2 * 2 * qtok * count * 2 * width
    packed = jax.ShapeDtypeStruct((qtok // 2, width + PACK), jnp.float32)
    return pl.pallas_call(
        attention_kernel,
        grid=(tiles,),
        in_specs=[
            pl.BlockSpec((TQ, width), lambda i: (i, 0)),
            pl.BlockSpec((count, width), lambda i: (0, 0)),
            pl.BlockSpec((count, width), lambda i: (0, 0)),
            pl.BlockSpec((1, count), lambda i: (0, 0)),
        ],
        out_specs=[
            pl.BlockSpec((TQ, width + PACK), lambda i: (jnp.minimum(i, half - 1), 0)),
            pl.BlockSpec((TQ, width + PACK), lambda i: (jnp.maximum(i - half, 0), 0)),
        ],
        out_shape=[packed, packed],
        cost_estimate=pl.CostEstimate(
            flops=flops,
            transcendentals=qtok * count * HEADS,
            bytes_accessed=qtok * width * 6 + count * width * 4,
        ),
    )(query_rows, keys, values, keep)


def merge_kernel(a_ref, b_ref, *out_refs):
    width = a_ref.shape[1] - PACK
    sa = a_ref[:, pl.ds(width, PACK)]
    sb = b_ref[:, pl.ds(width, PACK)]
    stat_lane = lax.broadcasted_iota(jnp.int32, (1, PACK), 1)
    top = jnp.maximum(sa, sb)
    fa = jnp.exp(sa - top)
    fb = jnp.exp(sb - top)
    heads_a = [jnp.sum(jnp.where(stat_lane == h, fa, 0.0), axis=1, keepdims=True) for h in range(HEADS)]
    heads_b = [jnp.sum(jnp.where(stat_lane == h, fb, 0.0), axis=1, keepdims=True) for h in range(HEADS)]
    spread_a = jnp.zeros_like(sa)
    spread_b = jnp.zeros_like(sb)
    for h in range(HEADS):
        spread_a = jnp.where(stat_lane == HEADS + h, heads_a[h], spread_a)
        spread_b = jnp.where(stat_lane == HEADS + h, heads_b[h], spread_b)
    tot = sa * spread_a + sb * spread_b
    stats = jnp.where(
        stat_lane < HEADS, top, jnp.where(stat_lane < 2 * HEADS, tot, jnp.float32(0.0))
    )
    lane = lax.broadcasted_iota(jnp.int32, (1, 2 * HD), 1)
    low = lane < HD
    blocks = []
    for pair in range(HEADS // 2):
        cols = pl.ds(pair * 2 * HD, 2 * HD)
        f_a = jnp.where(low, heads_a[2 * pair], heads_a[2 * pair + 1])
        f_b = jnp.where(low, heads_b[2 * pair], heads_b[2 * pair + 1])
        blocks.append(a_ref[:, cols] * f_a + b_ref[:, cols] * f_b)
    merged = jnp.concatenate(blocks + [stats], axis=1)
    if len(out_refs) == 1:
        out_refs[0][...] = merged
    else:
        half = merged.shape[0] // 2
        out_refs[0][...] = merged[:half]
        out_refs[1][...] = merged[half:]


def merge(kept, got, split):
    rows, cols = kept.shape
    count = 2 if split else 1
    shape = jax.ShapeDtypeStruct((rows // count, cols), jnp.float32)
    return pl.pallas_call(
        merge_kernel,
        out_shape=[shape] * count,
        cost_estimate=pl.CostEstimate(
            flops=4 * rows * cols, transcendentals=2 * rows * PACK, bytes_accessed=12 * rows * cols
        ),
    )(kept, got)


def step_bits(nbits):
    return [0, 1, 3, 2, 4] if nbits == 5 else list(range(nbits))


def block_order(groups):
    nbits = groups.bit_length() - 1
    me = lax.axis_index("tm")
    order = step_bits(nbits)
    pos = jnp.arange(groups, dtype=jnp.int32)
    block = jnp.zeros_like(pos)
    for i, bit in enumerate(order):
        a = (pos >> (nbits - 1 - i)) & 1
        block = block + ((a ^ ((me >> bit) & 1)) << bit)
    return block


def tree_reduce(first, second):
    groups = lax.axis_size("tm")
    nbits = groups.bit_length() - 1
    order = step_bits(nbits)
    for i, bit in enumerate(order):
        pairs = [(t, t ^ (1 << bit)) for t in range(groups)]
        got = lax.ppermute(second, "tm", pairs)
        last = i == len(order) - 1
        outs = merge(first, got, not last)
        if last:
            return outs[0]
        first, second = outs


def local(queries, kv_blocks, block_list, block_valid, w_out):
    hood = neighbourhood(kv_blocks)
    frames = hood.shape[1]
    nblk = hood.shape[4]
    blk = hood.shape[5]
    width = hood.shape[6]
    hood = hood.reshape(2, frames, 9 * nblk, blk, width)
    listed = block_list[0, 0]
    nlist = listed.shape[0]
    chosen = jnp.take(hood, listed, axis=2)
    keep = jnp.broadcast_to((block_valid[0, 0] > 0)[None, :, None], (frames, nlist, blk))
    keep = keep.reshape(1, -1).astype(jnp.int32)
    keys = chosen[0].reshape(-1, width)
    values = chosen[1].reshape(-1, width)
    query_rows = queries[0, 0]
    qtok = query_rows.shape[0]
    groups = lax.axis_size("tm")
    order = block_order(groups)
    query_rows = jnp.take(query_rows.reshape(groups, qtok // groups, width), order, axis=0)
    query_rows = query_rows.reshape(qtok, width)
    first, second = attention(query_rows, keys, values, keep)
    final = tree_reduce(first, second)
    summed = final[:, :width]
    total = final[:, width + HEADS : width + 2 * HEADS]
    own_rows = summed.shape[0]
    attended = summed / jnp.repeat(total, HD, axis=1)
    normed = attended * lax.rsqrt(jnp.mean(attended * attended, axis=1, keepdims=True) + 1e-06)
    normed = normed.astype(jnp.bfloat16)
    joined = jnp.dot(normed, w_out, preferred_element_type=jnp.float32)
    return joined.reshape(1, 1, own_rows, width)


def solution(mesh):
    in_specs = (
        P("height", "width", None, None),
        P(None, "tm", "height", "width", None, None, None),
        P("height", "width", None),
        P("height", "width", None),
        P(),
    )
    out_specs = P("height", "width", "tm", None)
    return jax.shard_map(local, mesh=mesh, in_specs=in_specs, out_specs=out_specs, check_vma=False)
```

```python
import jax
import jax.numpy as jnp
from jax import lax
from jax.experimental import pallas as pl
from jax.experimental.pallas import tpu as pltpu
from jax.sharding import PartitionSpec as P

HEADS = 8
HD = 64
TQ = 256


def shifted(array, axis, forward):
    size = lax.axis_size(axis)
    if forward:
        pairs = [(i, i + 1) for i in range(size - 1)]
    else:
        pairs = [(i + 1, i) for i in range(size - 1)]
    return lax.ppermute(array, axis, pairs)


def neighbourhood(kv_blocks):
    left = shifted(kv_blocks, "width", True)
    right = shifted(kv_blocks, "width", False)
    up_mid = shifted(kv_blocks, "height", True)
    down_mid = shifted(kv_blocks, "height", False)
    left, right, up_mid, down_mid = lax.optimization_barrier((left, right, up_mid, down_mid))
    sides = jnp.concatenate([left, right], axis=3)
    up_sides = shifted(sides, "height", True)
    down_sides = shifted(sides, "height", False)
    row = jnp.concatenate([left, kv_blocks, right], axis=3)
    up = jnp.concatenate([up_sides[:, :, :, :1], up_mid, up_sides[:, :, :, 1:]], axis=3)
    down = jnp.concatenate([down_sides[:, :, :, :1], down_mid, down_sides[:, :, :, 1:]], axis=3)
    return jnp.concatenate([up, row, down], axis=2)


PACK = 128


def encode_stats(stats):
    lane = lax.broadcasted_iota(jnp.int32, (1, PACK), 1)
    used = lane < 2 * HEADS
    hi = stats.astype(jnp.bfloat16).astype(jnp.float32)
    rest = stats - hi
    mid = rest.astype(jnp.bfloat16).astype(jnp.float32)
    lo = rest - mid
    zero = jnp.float32(0.0)
    coded = (
        jnp.where(used, hi, zero)
        + pltpu.roll(jnp.where(used, mid, zero), 2 * HEADS, 1)
        + pltpu.roll(jnp.where(used, lo, zero), 4 * HEADS, 1)
    )
    return coded.astype(jnp.bfloat16)


def decode_stats(coded):
    lane = lax.broadcasted_iota(jnp.int32, (1, PACK), 1)
    used = lane < 2 * HEADS
    wide = coded.astype(jnp.float32)
    zero = jnp.float32(0.0)
    hi = jnp.where(used, wide, zero)
    mid = jnp.where(used, pltpu.roll(wide, PACK - 2 * HEADS, 1), zero)
    lo = jnp.where(used, pltpu.roll(wide, PACK - 4 * HEADS, 1), zero)
    return (hi + mid) + lo


def attention_kernel(q_ref, k_ref, v_ref, keep_ref, first_ref, second_ref):
    rows = q_ref.shape[0]
    step = pl.program_id(0)
    half = pl.num_programs(0) // 2
    keep = keep_ref[...] > 0
    lane = lax.broadcasted_iota(jnp.int32, (1, 2 * HD), 1)
    low = lane < HD
    stat_lane = lax.broadcasted_iota(jnp.int32, (1, PACK), 1)
    stats = jnp.zeros((rows, PACK), jnp.float32)
    blocks = []
    for pair in range(HEADS // 2):
        cols = pl.ds(pair * 2 * HD, 2 * HD)
        q2 = q_ref[:, cols]
        k2 = k_ref[:, cols]
        v2 = v_ref[:, cols]
        outs = []
        for part in range(2):
            mine = low if part == 0 else jnp.logical_not(low)
            qh = jnp.where(mine, q2, jnp.zeros_like(q2))
            scores = lax.dot_general(
                qh, k2, (((1,), (1,)), ((), ())), preferred_element_type=jnp.float32
            )
            scores = scores / jnp.float32(8.0)
            scores = jnp.where(keep, scores, jnp.float32(-1e30))
            top = jnp.max(scores, axis=1, keepdims=True)
            probs = jnp.where(keep, jnp.exp(scores - top), jnp.float32(0.0))
            total = jnp.sum(probs, axis=1, keepdims=True)
            outs.append(
                jnp.dot(probs.astype(jnp.bfloat16), v2, preferred_element_type=jnp.float32)
            )
            head = pair * 2 + part
            stats = jnp.where(stat_lane == head, top, stats)
            stats = jnp.where(stat_lane == HEADS + head, total, stats)
        blocks.append(jnp.where(low, outs[0], outs[1]))
    @pl.when(step < half)
    def _():
        first_ref[...] = jnp.concatenate(blocks + [stats], axis=1)

    @pl.when(step >= half)
    def _():
        sent = [b.astype(jnp.bfloat16) for b in blocks]
        second_ref[...] = jnp.concatenate(sent + [encode_stats(stats)], axis=1)


def attention(query_rows, keys, values, keep):
    qtok, width = query_rows.shape
    count = keys.shape[0]
    tiles = qtok // TQ
    half = tiles // 2
    flops = 2 * 2 * qtok * count * 2 * width
    packed = jax.ShapeDtypeStruct((qtok // 2, width + PACK), jnp.float32)
    sent = jax.ShapeDtypeStruct((qtok // 2, width + PACK), jnp.bfloat16)
    return pl.pallas_call(
        attention_kernel,
        grid=(tiles,),
        in_specs=[
            pl.BlockSpec((TQ, width), lambda i: (i, 0)),
            pl.BlockSpec((count, width), lambda i: (0, 0)),
            pl.BlockSpec((count, width), lambda i: (0, 0)),
            pl.BlockSpec((1, count), lambda i: (0, 0)),
        ],
        out_specs=[
            pl.BlockSpec((TQ, width + PACK), lambda i: (jnp.minimum(i, half - 1), 0)),
            pl.BlockSpec((TQ, width + PACK), lambda i: (jnp.maximum(i - half, 0), 0)),
        ],
        out_shape=[packed, sent],
        cost_estimate=pl.CostEstimate(
            flops=flops,
            transcendentals=qtok * count * HEADS,
            bytes_accessed=qtok * width * 6 + count * width * 4,
        ),
    )(query_rows, keys, values, keep)


def merge_kernel(a_ref, b_ref, *out_refs):
    width = a_ref.shape[1] - PACK
    sa = a_ref[:, pl.ds(width, PACK)]
    sb = decode_stats(b_ref[:, pl.ds(width, PACK)])
    stat_lane = lax.broadcasted_iota(jnp.int32, (1, PACK), 1)
    top = jnp.maximum(sa, sb)
    fa = jnp.exp(sa - top)
    fb = jnp.exp(sb - top)
    heads_a = [jnp.sum(jnp.where(stat_lane == h, fa, 0.0), axis=1, keepdims=True) for h in range(HEADS)]
    heads_b = [jnp.sum(jnp.where(stat_lane == h, fb, 0.0), axis=1, keepdims=True) for h in range(HEADS)]
    spread_a = jnp.zeros_like(sa)
    spread_b = jnp.zeros_like(sb)
    for h in range(HEADS):
        spread_a = jnp.where(stat_lane == HEADS + h, heads_a[h], spread_a)
        spread_b = jnp.where(stat_lane == HEADS + h, heads_b[h], spread_b)
    tot = sa * spread_a + sb * spread_b
    stats = jnp.where(
        stat_lane < HEADS, top, jnp.where(stat_lane < 2 * HEADS, tot, jnp.float32(0.0))
    )
    lane = lax.broadcasted_iota(jnp.int32, (1, 2 * HD), 1)
    low = lane < HD
    blocks = []
    for pair in range(HEADS // 2):
        cols = pl.ds(pair * 2 * HD, 2 * HD)
        f_a = jnp.where(low, heads_a[2 * pair], heads_a[2 * pair + 1])
        f_b = jnp.where(low, heads_b[2 * pair], heads_b[2 * pair + 1])
        blocks.append(a_ref[:, cols] * f_a + b_ref[:, cols].astype(jnp.float32) * f_b)
    if len(out_refs) == 1:
        out_refs[0][...] = jnp.concatenate(blocks + [stats], axis=1)
    else:
        half = stats.shape[0] // 2
        out_refs[0][...] = jnp.concatenate([b[:half] for b in blocks] + [stats[:half]], axis=1)
        sent = [b[half:].astype(jnp.bfloat16) for b in blocks]
        out_refs[1][...] = jnp.concatenate(sent + [encode_stats(stats[half:])], axis=1)


def merge(kept, got, split):
    rows, cols = kept.shape
    count = 2 if split else 1
    shape = jax.ShapeDtypeStruct((rows // count, cols), jnp.float32)
    shapes = [shape, jax.ShapeDtypeStruct(shape.shape, jnp.bfloat16)] if split else [shape]
    return pl.pallas_call(
        merge_kernel,
        out_shape=shapes,
        cost_estimate=pl.CostEstimate(
            flops=4 * rows * cols, transcendentals=2 * rows * PACK, bytes_accessed=12 * rows * cols
        ),
    )(kept, got)


def step_bits(nbits):
    return [0, 1, 3, 2, 4] if nbits == 5 else list(range(nbits))


def block_order(groups):
    nbits = groups.bit_length() - 1
    me = lax.axis_index("tm")
    order = step_bits(nbits)
    pos = jnp.arange(groups, dtype=jnp.int32)
    block = jnp.zeros_like(pos)
    for i, bit in enumerate(order):
        a = (pos >> (nbits - 1 - i)) & 1
        block = block + ((a ^ ((me >> bit) & 1)) << bit)
    return block


def tree_reduce(first, second):
    groups = lax.axis_size("tm")
    nbits = groups.bit_length() - 1
    order = step_bits(nbits)
    for i, bit in enumerate(order):
        pairs = [(t, t ^ (1 << bit)) for t in range(groups)]
        got = lax.ppermute(second, "tm", pairs)
        last = i == len(order) - 1
        outs = merge(first, got, not last)
        if last:
            return outs[0]
        first, second = outs


def local(queries, kv_blocks, block_list, block_valid, w_out):
    hood = neighbourhood(kv_blocks)
    frames = hood.shape[1]
    nblk = hood.shape[4]
    blk = hood.shape[5]
    width = hood.shape[6]
    hood = hood.reshape(2, frames, 9 * nblk, blk, width)
    listed = block_list[0, 0]
    nlist = listed.shape[0]
    chosen = jnp.take(hood, listed, axis=2)
    keep = jnp.broadcast_to((block_valid[0, 0] > 0)[None, :, None], (frames, nlist, blk))
    keep = keep.reshape(1, -1).astype(jnp.int32)
    keys = chosen[0].reshape(-1, width)
    values = chosen[1].reshape(-1, width)
    query_rows = queries[0, 0]
    qtok = query_rows.shape[0]
    groups = lax.axis_size("tm")
    order = block_order(groups)
    query_rows = jnp.take(query_rows.reshape(groups, qtok // groups, width), order, axis=0)
    query_rows = query_rows.reshape(qtok, width)
    first, second = attention(query_rows, keys, values, keep)
    final = tree_reduce(first, second)
    summed = final[:, :width]
    total = final[:, width + HEADS : width + 2 * HEADS]
    own_rows = summed.shape[0]
    attended = summed / jnp.repeat(total, HD, axis=1)
    normed = attended * lax.rsqrt(jnp.mean(attended * attended, axis=1, keepdims=True) + 1e-06)
    normed = normed.astype(jnp.bfloat16)
    joined = jnp.dot(normed, w_out, preferred_element_type=jnp.float32)
    return joined.reshape(1, 1, own_rows, width)


def solution(mesh):
    in_specs = (
        P("height", "width", None, None),
        P(None, "tm", "height", "width", None, None, None),
        P("height", "width", None),
        P("height", "width", None),
        P(),
    )
    out_specs = P("height", "width", "tm", None)
    return jax.shard_map(local, mesh=mesh, in_specs=in_specs, out_specs=out_specs, check_vma=False)
```

```python
import jax
import jax.numpy as jnp
from jax import lax
from jax.experimental import pallas as pl
from jax.experimental.pallas import tpu as pltpu
from jax.sharding import PartitionSpec as P

HEADS = 8
HD = 64
TQ = 256


def shifted(array, axis, forward):
    size = lax.axis_size(axis)
    if forward:
        pairs = [(i, i + 1) for i in range(size - 1)]
    else:
        pairs = [(i + 1, i) for i in range(size - 1)]
    return lax.ppermute(array, axis, pairs)


def neighbourhood(kv_blocks):
    left = shifted(kv_blocks, "width", True)
    right = shifted(kv_blocks, "width", False)
    up_mid = shifted(kv_blocks, "height", True)
    down_mid = shifted(kv_blocks, "height", False)
    left, right, up_mid, down_mid = lax.optimization_barrier((left, right, up_mid, down_mid))
    sides = jnp.concatenate([left, right], axis=3)
    up_sides = shifted(sides, "height", True)
    down_sides = shifted(sides, "height", False)
    row = jnp.concatenate([left, kv_blocks, right], axis=3)
    up = jnp.concatenate([up_sides[:, :, :, :1], up_mid, up_sides[:, :, :, 1:]], axis=3)
    down = jnp.concatenate([down_sides[:, :, :, :1], down_mid, down_sides[:, :, :, 1:]], axis=3)
    return jnp.concatenate([up, row, down], axis=2)


PACK = 128


def attention_kernel(q_ref, k_ref, v_ref, keep_ref, first_ref, second_ref):
    rows = q_ref.shape[0]
    step = pl.program_id(0)
    half = pl.num_programs(0) // 2
    keep = keep_ref[...] > 0
    lane = lax.broadcasted_iota(jnp.int32, (1, 2 * HD), 1)
    low = lane < HD
    stat_lane = lax.broadcasted_iota(jnp.int32, (1, PACK), 1)
    stats = jnp.zeros((rows, PACK), jnp.float32)
    blocks = []
    for pair in range(HEADS // 2):
        cols = pl.ds(pair * 2 * HD, 2 * HD)
        q2 = q_ref[:, cols]
        k2 = k_ref[:, cols]
        v2 = v_ref[:, cols]
        outs = []
        for part in range(2):
            mine = low if part == 0 else jnp.logical_not(low)
            qh = jnp.where(mine, q2, jnp.zeros_like(q2))
            scores = lax.dot_general(
                qh, k2, (((1,), (1,)), ((), ())), preferred_element_type=jnp.float32
            )
            scores = scores / jnp.float32(8.0)
            scores = jnp.where(keep, scores, jnp.float32(-1e30))
            top = jnp.max(scores, axis=1, keepdims=True)
            probs = jnp.where(keep, jnp.exp(scores - top), jnp.float32(0.0))
            total = jnp.sum(probs, axis=1, keepdims=True)
            outs.append(
                jnp.dot(probs.astype(jnp.bfloat16), v2, preferred_element_type=jnp.float32)
            )
            head = pair * 2 + part
            stats = jnp.where(stat_lane == head, top, stats)
            stats = jnp.where(stat_lane == HEADS + head, total, stats)
        blocks.append(jnp.where(low, outs[0], outs[1]))
    packed = jnp.concatenate(blocks + [stats], axis=1)

    @pl.when(step < half)
    def _():
        first_ref[...] = packed

    @pl.when(step >= half)
    def _():
        second_ref[...] = packed


def attention(query_rows, keys, values, keep):
    qtok, width = query_rows.shape
    count = keys.shape[0]
    tiles = qtok // TQ
    half = tiles // 2
    flops = 2 * 2 * qtok * count * 2 * width
    packed = jax.ShapeDtypeStruct((qtok // 2, width + PACK), jnp.float32)
    return pl.pallas_call(
        attention_kernel,
        grid=(tiles,),
        in_specs=[
            pl.BlockSpec((TQ, width), lambda i: (i, 0)),
            pl.BlockSpec((count, width), lambda i: (0, 0)),
            pl.BlockSpec((count, width), lambda i: (0, 0)),
            pl.BlockSpec((1, count), lambda i: (0, 0)),
        ],
        out_specs=[
            pl.BlockSpec((TQ, width + PACK), lambda i: (jnp.minimum(i, half - 1), 0)),
            pl.BlockSpec((TQ, width + PACK), lambda i: (jnp.maximum(i - half, 0), 0)),
        ],
        out_shape=[packed, packed],
        cost_estimate=pl.CostEstimate(
            flops=flops,
            transcendentals=qtok * count * HEADS,
            bytes_accessed=qtok * width * 6 + count * width * 4,
        ),
    )(query_rows, keys, values, keep)


def merge_kernel(a_ref, b_ref, *out_refs):
    width = a_ref.shape[1] - PACK
    sa = a_ref[:, pl.ds(width, PACK)]
    sb = b_ref[:, pl.ds(width, PACK)]
    stat_lane = lax.broadcasted_iota(jnp.int32, (1, PACK), 1)
    top = jnp.maximum(sa, sb)
    fa = jnp.exp(sa - top)
    fb = jnp.exp(sb - top)
    heads_a = [jnp.sum(jnp.where(stat_lane == h, fa, 0.0), axis=1, keepdims=True) for h in range(HEADS)]
    heads_b = [jnp.sum(jnp.where(stat_lane == h, fb, 0.0), axis=1, keepdims=True) for h in range(HEADS)]
    spread_a = jnp.zeros_like(sa)
    spread_b = jnp.zeros_like(sb)
    for h in range(HEADS):
        spread_a = jnp.where(stat_lane == HEADS + h, heads_a[h], spread_a)
        spread_b = jnp.where(stat_lane == HEADS + h, heads_b[h], spread_b)
    tot = sa * spread_a + sb * spread_b
    stats = jnp.where(
        stat_lane < HEADS, top, jnp.where(stat_lane < 2 * HEADS, tot, jnp.float32(0.0))
    )
    lane = lax.broadcasted_iota(jnp.int32, (1, 2 * HD), 1)
    low = lane < HD
    blocks = []
    for pair in range(HEADS // 2):
        cols = pl.ds(pair * 2 * HD, 2 * HD)
        f_a = jnp.where(low, heads_a[2 * pair], heads_a[2 * pair + 1])
        f_b = jnp.where(low, heads_b[2 * pair], heads_b[2 * pair + 1])
        blocks.append(a_ref[:, cols] * f_a + b_ref[:, cols] * f_b)
    merged = jnp.concatenate(blocks + [stats], axis=1)
    if len(out_refs) == 1:
        out_refs[0][...] = merged
    else:
        half = merged.shape[0] // 2
        out_refs[0][...] = merged[:half]
        out_refs[1][...] = merged[half:]


def merge(kept, got, split):
    rows, cols = kept.shape
    count = 2 if split else 1
    shape = jax.ShapeDtypeStruct((rows // count, cols), jnp.float32)
    return pl.pallas_call(
        merge_kernel,
        out_shape=[shape] * count,
        cost_estimate=pl.CostEstimate(
            flops=4 * rows * cols, transcendentals=2 * rows * PACK, bytes_accessed=12 * rows * cols
        ),
    )(kept, got)


def step_bits(nbits, core):
    if nbits != 5:
        return [jnp.int32(b) for b in range(nbits)]
    first, second = [0, 1, 3, 2, 4], [0, 3, 1, 4, 2]
    return [jnp.where(core == 0, a, b) for a, b in zip(first, second)]


def step_pairs(nbits, step):
    pairs = []
    for t in range(1 << nbits):
        bits = [0, 1, 3, 2, 4] if t % 2 == 0 else [0, 3, 1, 4, 2]
        bit = bits[step] if nbits == 5 else step
        pairs.append((t, t ^ (1 << bit)))
    return pairs


def block_order(groups, me):
    nbits = groups.bit_length() - 1
    order = step_bits(nbits, me & 1)
    pos = jnp.arange(groups, dtype=jnp.int32)
    block = jnp.zeros_like(pos)
    for i, bit in enumerate(order):
        a = (pos >> (nbits - 1 - i)) & 1
        block = block + ((a ^ ((me >> bit) & 1)) << bit)
    return block


def tree_reduce(first, second):
    groups = lax.axis_size("tm")
    nbits = groups.bit_length() - 1
    for i in range(nbits):
        got = lax.ppermute(second, "tm", step_pairs(nbits, i))
        last = i == nbits - 1
        outs = merge(first, got, not last)
        if last:
            return outs[0]
        first, second = outs


def local(queries, kv_blocks, block_list, block_valid, w_out):
    hood = neighbourhood(kv_blocks)
    frames = hood.shape[1]
    nblk = hood.shape[4]
    blk = hood.shape[5]
    width = hood.shape[6]
    hood = hood.reshape(2, frames, 9 * nblk, blk, width)
    listed = block_list[0, 0]
    nlist = listed.shape[0]
    chosen = jnp.take(hood, listed, axis=2)
    keep = jnp.broadcast_to((block_valid[0, 0] > 0)[None, :, None], (frames, nlist, blk))
    keep = keep.reshape(1, -1).astype(jnp.int32)
    keys = chosen[0].reshape(-1, width)
    values = chosen[1].reshape(-1, width)
    query_rows = queries[0, 0]
    qtok = query_rows.shape[0]
    groups = lax.axis_size("tm")
    me = lax.axis_index("tm")
    order = jnp.concatenate(
        [block_order(groups, me)[: groups // 2], block_order(groups, me ^ 1)[: groups // 2]]
    )
    query_rows = jnp.take(query_rows.reshape(groups, qtok // groups, width), order, axis=0)
    query_rows = query_rows.reshape(qtok, width)
    first, second = attention(query_rows, keys, values, keep)
    final = tree_reduce(first, second)
    summed = final[:, :width]
    total = final[:, width + HEADS : width + 2 * HEADS]
    own_rows = summed.shape[0]
    attended = summed / jnp.repeat(total, HD, axis=1)
    normed = attended * lax.rsqrt(jnp.mean(attended * attended, axis=1, keepdims=True) + 1e-06)
    normed = normed.astype(jnp.bfloat16)
    joined = jnp.dot(normed, w_out, preferred_element_type=jnp.float32)
    return joined.reshape(1, 1, own_rows, width)


def solution(mesh):
    in_specs = (
        P("height", "width", None, None),
        P(None, "tm", "height", "width", None, None, None),
        P("height", "width", None),
        P("height", "width", None),
        P(),
    )
    out_specs = P("height", "width", "tm", None)
    return jax.shard_map(local, mesh=mesh, in_specs=in_specs, out_specs=out_specs, check_vma=False)
```

```python
import jax
import jax.numpy as jnp
from jax import lax
from jax.experimental import pallas as pl
from jax.experimental.pallas import tpu as pltpu
from jax.sharding import PartitionSpec as P

HEADS = 8
HD = 64
TQ = 256


def shifted(array, axis, forward):
    size = lax.axis_size(axis)
    if forward:
        pairs = [(i, i + 1) for i in range(size - 1)]
    else:
        pairs = [(i + 1, i) for i in range(size - 1)]
    return lax.ppermute(array, axis, pairs)


def neighbourhood(kv_blocks):
    left = shifted(kv_blocks, "width", True)
    right = shifted(kv_blocks, "width", False)
    up_mid = shifted(kv_blocks, "height", True)
    down_mid = shifted(kv_blocks, "height", False)
    left, right, up_mid, down_mid = lax.optimization_barrier((left, right, up_mid, down_mid))
    sides = jnp.concatenate([left, right], axis=3)
    up_sides = shifted(sides, "height", True)
    down_sides = shifted(sides, "height", False)
    row = jnp.concatenate([left, kv_blocks, right], axis=3)
    up = jnp.concatenate([up_sides[:, :, :, :1], up_mid, up_sides[:, :, :, 1:]], axis=3)
    down = jnp.concatenate([down_sides[:, :, :, :1], down_mid, down_sides[:, :, :, 1:]], axis=3)
    return jnp.concatenate([up, row, down], axis=2)


PACK = 128


def attention_kernel(q_ref, k_ref, v_ref, keep_ref, out_ref):
    rows = q_ref.shape[0]
    keep = keep_ref[...] > 0
    lane = lax.broadcasted_iota(jnp.int32, (1, 2 * HD), 1)
    low = lane < HD
    stat_lane = lax.broadcasted_iota(jnp.int32, (1, PACK), 1)
    stats = jnp.zeros((rows, PACK), jnp.float32)
    scale = jnp.asarray(1.0 / 8.0, jnp.bfloat16)
    blocks = []
    for pair in range(HEADS // 2):
        cols = pl.ds(pair * 2 * HD, 2 * HD)
        q2 = q_ref[:, cols] * scale
        k2 = k_ref[:, cols]
        v2 = v_ref[:, cols]
        outs = []
        for part in range(2):
            mine = low if part == 0 else jnp.logical_not(low)
            qh = jnp.where(mine, q2, jnp.zeros_like(q2))
            scores = lax.dot_general(
                qh, k2, (((1,), (1,)), ((), ())), preferred_element_type=jnp.float32
            )
            scores = jnp.where(keep, scores, jnp.float32(-1e30))
            top = jnp.max(scores, axis=1, keepdims=True)
            probs = jnp.exp(scores - top)
            total = jnp.sum(probs, axis=1, keepdims=True)
            outs.append(
                jnp.dot(probs.astype(jnp.bfloat16), v2, preferred_element_type=jnp.float32)
            )
            head = pair * 2 + part
            stats = jnp.where(stat_lane == head, top, stats)
            stats = jnp.where(stat_lane == HEADS + head, total, stats)
        blocks.append(jnp.where(low, outs[0], outs[1]))
    out_ref[...] = jnp.concatenate(blocks + [stats], axis=1)


def attention(query_rows, keys, values, keep):
    qtok, width = query_rows.shape
    count = keys.shape[0]
    tiles = qtok // TQ
    flops = 2 * 2 * qtok * count * 2 * width
    return pl.pallas_call(
        attention_kernel,
        grid=(tiles,),
        in_specs=[
            pl.BlockSpec((TQ, width), lambda i: (i, 0)),
            pl.BlockSpec((count, width), lambda i: (0, 0)),
            pl.BlockSpec((count, width), lambda i: (0, 0)),
            pl.BlockSpec((1, count), lambda i: (0, 0)),
        ],
        out_specs=pl.BlockSpec((TQ, width + PACK), lambda i: (i, 0)),
        out_shape=jax.ShapeDtypeStruct((qtok, width + PACK), jnp.float32),
        cost_estimate=pl.CostEstimate(
            flops=flops,
            transcendentals=qtok * count * HEADS,
            bytes_accessed=qtok * width * 6 + count * width * 4,
        ),
    )(query_rows, keys, values, keep)


def merge_kernel(a_ref, b_ref, *out_refs):
    width = a_ref.shape[1] - PACK
    sa = a_ref[:, pl.ds(width, PACK)]
    sb = b_ref[:, pl.ds(width, PACK)]
    stat_lane = lax.broadcasted_iota(jnp.int32, (1, PACK), 1)
    top = jnp.maximum(sa, sb)
    fa = jnp.exp(sa - top)
    fb = jnp.exp(sb - top)
    heads_a = [jnp.sum(jnp.where(stat_lane == h, fa, 0.0), axis=1, keepdims=True) for h in range(HEADS)]
    heads_b = [jnp.sum(jnp.where(stat_lane == h, fb, 0.0), axis=1, keepdims=True) for h in range(HEADS)]
    spread_a = jnp.zeros_like(sa)
    spread_b = jnp.zeros_like(sb)
    for h in range(HEADS):
        spread_a = jnp.where(stat_lane == HEADS + h, heads_a[h], spread_a)
        spread_b = jnp.where(stat_lane == HEADS + h, heads_b[h], spread_b)
    tot = sa * spread_a + sb * spread_b
    stats = jnp.where(
        stat_lane < HEADS, top, jnp.where(stat_lane < 2 * HEADS, tot, jnp.float32(0.0))
    )
    lane = lax.broadcasted_iota(jnp.int32, (1, 2 * HD), 1)
    low = lane < HD
    blocks = []
    for pair in range(HEADS // 2):
        cols = pl.ds(pair * 2 * HD, 2 * HD)
        f_a = jnp.where(low, heads_a[2 * pair], heads_a[2 * pair + 1])
        f_b = jnp.where(low, heads_b[2 * pair], heads_b[2 * pair + 1])
        blocks.append(a_ref[:, cols] * f_a + b_ref[:, cols] * f_b)
    merged = jnp.concatenate(blocks + [stats], axis=1)
    if len(out_refs) == 1:
        out_refs[0][...] = merged
    else:
        half = merged.shape[0] // 2
        out_refs[0][...] = merged[:half]
        out_refs[1][...] = merged[half:]


def merge(kept, got, split):
    rows, cols = kept.shape
    count = 2 if split else 1
    shape = jax.ShapeDtypeStruct((rows // count, cols), jnp.float32)
    return pl.pallas_call(
        merge_kernel,
        out_shape=[shape] * count,
        cost_estimate=pl.CostEstimate(
            flops=4 * rows * cols, transcendentals=2 * rows * PACK, bytes_accessed=12 * rows * cols
        ),
    )(kept, got)


def step_bits(nbits, core):
    if nbits != 5:
        return [jnp.int32(b) for b in range(nbits)]
    first, second = [0, 1, 3, 2, 4], [0, 3, 1, 4, 2]
    return [jnp.where(core == 0, a, b) for a, b in zip(first, second)]


def step_pairs(nbits, step):
    pairs = []
    for t in range(1 << nbits):
        bits = [0, 1, 3, 2, 4] if t % 2 == 0 else [0, 3, 1, 4, 2]
        bit = bits[step] if nbits == 5 else step
        pairs.append((t, t ^ (1 << bit)))
    return pairs


def block_order(groups, me):
    nbits = groups.bit_length() - 1
    order = step_bits(nbits, me & 1)
    pos = jnp.arange(groups, dtype=jnp.int32)
    block = jnp.zeros_like(pos)
    for i, bit in enumerate(order):
        a = (pos >> (nbits - 1 - i)) & 1
        block = block + ((a ^ ((me >> bit) & 1)) << bit)
    return block


def tree_reduce(first, second):
    groups = lax.axis_size("tm")
    nbits = groups.bit_length() - 1
    for i in range(nbits):
        got = lax.ppermute(second, "tm", step_pairs(nbits, i))
        last = i == nbits - 1
        outs = merge(first, got, not last)
        if last:
            return outs[0]
        first, second = outs


def local(queries, kv_blocks, block_list, block_valid, w_out):
    hood = neighbourhood(kv_blocks)
    frames = hood.shape[1]
    nblk = hood.shape[4]
    blk = hood.shape[5]
    width = hood.shape[6]
    hood = hood.reshape(2, frames, 9 * nblk, blk, width)
    listed = block_list[0, 0]
    nlist = listed.shape[0]
    chosen = jnp.take(hood, listed, axis=2)
    keep = jnp.broadcast_to((block_valid[0, 0] > 0)[None, :, None], (frames, nlist, blk))
    keep = keep.reshape(1, -1).astype(jnp.int32)
    keys = chosen[0].reshape(-1, width)
    values = chosen[1].reshape(-1, width)
    query_rows = queries[0, 0]
    qtok = query_rows.shape[0]
    groups = lax.axis_size("tm")
    me = lax.axis_index("tm")
    order = jnp.concatenate(
        [block_order(groups, me)[: groups // 2], block_order(groups, me ^ 1)[: groups // 2]]
    )
    query_rows = jnp.take(query_rows.reshape(groups, qtok // groups, width), order, axis=0)
    query_rows = query_rows.reshape(qtok, width)
    second = attention(query_rows[qtok // 2 :], keys, values, keep)
    first = attention(query_rows[: qtok // 2], keys, values, keep)
    final = tree_reduce(first, second)
    summed = final[:, :width]
    total = final[:, width + HEADS : width + 2 * HEADS]
    own_rows = summed.shape[0]
    attended = summed / jnp.repeat(total, HD, axis=1)
    normed = attended * lax.rsqrt(jnp.mean(attended * attended, axis=1, keepdims=True) + 1e-06)
    normed = normed.astype(jnp.bfloat16)
    joined = jnp.dot(normed, w_out, preferred_element_type=jnp.float32)
    return joined.reshape(1, 1, own_rows, width)


def solution(mesh):
    in_specs = (
        P("height", "width", None, None),
        P(None, "tm", "height", "width", None, None, None),
        P("height", "width", None),
        P("height", "width", None),
        P(),
    )
    out_specs = P("height", "width", "tm", None)
    return jax.shard_map(local, mesh=mesh, in_specs=in_specs, out_specs=out_specs, check_vma=False)
```

```python
import jax
import jax.numpy as jnp
from jax import lax
from jax.experimental import pallas as pl
from jax.experimental.pallas import tpu as pltpu
from jax.sharding import PartitionSpec as P

HEADS = 8
HD = 64
TQ = 256


def shifted(array, axis, forward):
    size = lax.axis_size(axis)
    if forward:
        pairs = [(i, i + 1) for i in range(size - 1)]
    else:
        pairs = [(i + 1, i) for i in range(size - 1)]
    return lax.ppermute(array, axis, pairs)


def neighbourhood(kv_blocks):
    left = shifted(kv_blocks, "width", True)
    right = shifted(kv_blocks, "width", False)
    up_mid = shifted(kv_blocks, "height", True)
    down_mid = shifted(kv_blocks, "height", False)
    left, right, up_mid, down_mid = lax.optimization_barrier((left, right, up_mid, down_mid))
    sides = jnp.concatenate([left, right], axis=3)
    up_sides = shifted(sides, "height", True)
    down_sides = shifted(sides, "height", False)
    row = jnp.concatenate([left, kv_blocks, right], axis=3)
    up = jnp.concatenate([up_sides[:, :, :, :1], up_mid, up_sides[:, :, :, 1:]], axis=3)
    down = jnp.concatenate([down_sides[:, :, :, :1], down_mid, down_sides[:, :, :, 1:]], axis=3)
    return jnp.concatenate([up, row, down], axis=2)


PACK = 128


def attention_kernel(qt_ref, k_ref, vt_ref, keep_ref, out_ref):
    rows = qt_ref.shape[1]
    keep = keep_ref[...] > 0
    sub = lax.broadcasted_iota(jnp.int32, (2 * HD, 1), 0)
    low = sub < HD
    stat_row = lax.broadcasted_iota(jnp.int32, (PACK, 1), 0)
    stats = jnp.zeros((PACK, rows), jnp.float32)
    scale = jnp.asarray(1.0 / 8.0, jnp.bfloat16)
    blocks = []
    for pair in range(HEADS // 2):
        dims = pl.ds(pair * 2 * HD, 2 * HD)
        qt2 = qt_ref[dims, :] * scale
        k2 = k_ref[:, dims]
        vt2 = vt_ref[dims, :]
        outs = []
        for part in range(2):
            mine = low if part == 0 else jnp.logical_not(low)
            qh = jnp.where(mine, qt2, jnp.zeros_like(qt2))
            scores = jnp.dot(k2, qh, preferred_element_type=jnp.float32)
            scores = jnp.where(keep, scores, jnp.float32(-1e30))
            top = jnp.max(scores, axis=0, keepdims=True)
            probs = jnp.exp(scores - top)
            total = jnp.sum(probs, axis=0, keepdims=True)
            outs.append(
                jnp.dot(vt2, probs.astype(jnp.bfloat16), preferred_element_type=jnp.float32)
            )
            head = pair * 2 + part
            stats = jnp.where(stat_row == head, top, stats)
            stats = jnp.where(stat_row == HEADS + head, total, stats)
        blocks.append(jnp.where(low, outs[0], outs[1]).T)
    out_ref[...] = jnp.concatenate(blocks + [stats.T], axis=1)


def attention(query_t, keys, values_t, keep, first, count_rows):
    width, qtok = query_t.shape
    count = keys.shape[0]
    tiles = count_rows // TQ
    offset = first // TQ
    flops = 2 * 2 * count_rows * count * 2 * width
    return pl.pallas_call(
        attention_kernel,
        grid=(tiles,),
        in_specs=[
            pl.BlockSpec((width, TQ), lambda i: (0, i + offset)),
            pl.BlockSpec((count, width), lambda i: (0, 0)),
            pl.BlockSpec((width, count), lambda i: (0, 0)),
            pl.BlockSpec((count, 1), lambda i: (0, 0)),
        ],
        out_specs=pl.BlockSpec((TQ, width + PACK), lambda i: (i, 0)),
        out_shape=jax.ShapeDtypeStruct((count_rows, width + PACK), jnp.float32),
        cost_estimate=pl.CostEstimate(
            flops=flops,
            transcendentals=count_rows * count * HEADS,
            bytes_accessed=count_rows * width * 6 + count * width * 4,
        ),
    )(query_t, keys, values_t, keep)


def merge_kernel(a_ref, b_ref, *out_refs):
    width = a_ref.shape[1] - PACK
    sa = a_ref[:, pl.ds(width, PACK)]
    sb = b_ref[:, pl.ds(width, PACK)]
    stat_lane = lax.broadcasted_iota(jnp.int32, (1, PACK), 1)
    top = jnp.maximum(sa, sb)
    fa = jnp.exp(sa - top)
    fb = jnp.exp(sb - top)
    heads_a = [jnp.sum(jnp.where(stat_lane == h, fa, 0.0), axis=1, keepdims=True) for h in range(HEADS)]
    heads_b = [jnp.sum(jnp.where(stat_lane == h, fb, 0.0), axis=1, keepdims=True) for h in range(HEADS)]
    spread_a = jnp.zeros_like(sa)
    spread_b = jnp.zeros_like(sb)
    for h in range(HEADS):
        spread_a = jnp.where(stat_lane == HEADS + h, heads_a[h], spread_a)
        spread_b = jnp.where(stat_lane == HEADS + h, heads_b[h], spread_b)
    tot = sa * spread_a + sb * spread_b
    stats = jnp.where(
        stat_lane < HEADS, top, jnp.where(stat_lane < 2 * HEADS, tot, jnp.float32(0.0))
    )
    lane = lax.broadcasted_iota(jnp.int32, (1, 2 * HD), 1)
    low = lane < HD
    blocks = []
    for pair in range(HEADS // 2):
        cols = pl.ds(pair * 2 * HD, 2 * HD)
        f_a = jnp.where(low, heads_a[2 * pair], heads_a[2 * pair + 1])
        f_b = jnp.where(low, heads_b[2 * pair], heads_b[2 * pair + 1])
        blocks.append(a_ref[:, cols] * f_a + b_ref[:, cols] * f_b)
    merged = jnp.concatenate(blocks + [stats], axis=1)
    if len(out_refs) == 1:
        out_refs[0][...] = merged
    else:
        half = merged.shape[0] // 2
        out_refs[0][...] = merged[:half]
        out_refs[1][...] = merged[half:]


def merge(kept, got, split):
    rows, cols = kept.shape
    count = 2 if split else 1
    shape = jax.ShapeDtypeStruct((rows // count, cols), jnp.float32)
    return pl.pallas_call(
        merge_kernel,
        out_shape=[shape] * count,
        cost_estimate=pl.CostEstimate(
            flops=4 * rows * cols, transcendentals=2 * rows * PACK, bytes_accessed=12 * rows * cols
        ),
    )(kept, got)


def step_bits(nbits, core):
    if nbits != 5:
        return [jnp.int32(b) for b in range(nbits)]
    first, second = [0, 1, 3, 2, 4], [0, 3, 1, 4, 2]
    return [jnp.where(core == 0, a, b) for a, b in zip(first, second)]


def step_pairs(nbits, step):
    pairs = []
    for t in range(1 << nbits):
        bits = [0, 1, 3, 2, 4] if t % 2 == 0 else [0, 3, 1, 4, 2]
        bit = bits[step] if nbits == 5 else step
        pairs.append((t, t ^ (1 << bit)))
    return pairs


def block_order(groups, me):
    nbits = groups.bit_length() - 1
    order = step_bits(nbits, me & 1)
    pos = jnp.arange(groups, dtype=jnp.int32)
    block = jnp.zeros_like(pos)
    for i, bit in enumerate(order):
        a = (pos >> (nbits - 1 - i)) & 1
        block = block + ((a ^ ((me >> bit) & 1)) << bit)
    return block


def tree_reduce(first, second):
    groups = lax.axis_size("tm")
    nbits = groups.bit_length() - 1
    for i in range(nbits):
        got = lax.ppermute(second, "tm", step_pairs(nbits, i))
        last = i == nbits - 1
        outs = merge(first, got, not last)
        if last:
            return outs[0]
        first, second = outs


def local(queries, kv_blocks, block_list, block_valid, w_out):
    hood = neighbourhood(kv_blocks)
    frames = hood.shape[1]
    nblk = hood.shape[4]
    blk = hood.shape[5]
    width = hood.shape[6]
    hood = hood.reshape(2, frames, 9 * nblk, blk, width)
    listed = block_list[0, 0]
    nlist = listed.shape[0]
    chosen = jnp.take(hood, listed, axis=2)
    keep = jnp.broadcast_to((block_valid[0, 0] > 0)[None, :, None], (frames, nlist, blk))
    keep = keep.reshape(-1, 1).astype(jnp.int32)
    keys = chosen[0].reshape(-1, width)
    values = chosen[1].reshape(-1, width)
    query_rows = queries[0, 0]
    qtok = query_rows.shape[0]
    groups = lax.axis_size("tm")
    me = lax.axis_index("tm")
    order = jnp.concatenate(
        [block_order(groups, me)[: groups // 2], block_order(groups, me ^ 1)[: groups // 2]]
    )
    query_rows = jnp.take(query_rows.reshape(groups, qtok // groups, width), order, axis=0)
    query_rows = query_rows.reshape(qtok, width)
    query_t = query_rows.T
    values_t = values.T
    second = attention(query_t, keys, values_t, keep, qtok // 2, qtok // 2)
    first = attention(query_t, keys, values_t, keep, 0, qtok // 2)
    final = tree_reduce(first, second)
    summed = final[:, :width]
    total = final[:, width + HEADS : width + 2 * HEADS]
    own_rows = summed.shape[0]
    attended = summed / jnp.repeat(total, HD, axis=1)
    normed = attended * lax.rsqrt(jnp.mean(attended * attended, axis=1, keepdims=True) + 1e-06)
    normed = normed.astype(jnp.bfloat16)
    joined = jnp.dot(normed, w_out, preferred_element_type=jnp.float32)
    return joined.reshape(1, 1, own_rows, width)


def solution(mesh):
    in_specs = (
        P("height", "width", None, None),
        P(None, "tm", "height", "width", None, None, None),
        P("height", "width", None),
        P("height", "width", None),
        P(),
    )
    out_specs = P("height", "width", "tm", None)
    return jax.shard_map(local, mesh=mesh, in_specs=in_specs, out_specs=out_specs, check_vma=False)
```

```python
import jax
import jax.numpy as jnp
from jax import lax
from jax.experimental import pallas as pl
from jax.experimental.pallas import tpu as pltpu
from jax.sharding import PartitionSpec as P

HEADS = 8
HD = 64
TQ = 256


def shifted(array, axis, forward):
    size = lax.axis_size(axis)
    if forward:
        pairs = [(i, i + 1) for i in range(size - 1)]
    else:
        pairs = [(i + 1, i) for i in range(size - 1)]
    return lax.ppermute(array, axis, pairs)


def neighbourhood(kv_blocks):
    left = shifted(kv_blocks, "width", True)
    right = shifted(kv_blocks, "width", False)
    up_mid = shifted(kv_blocks, "height", True)
    down_mid = shifted(kv_blocks, "height", False)
    left, right, up_mid, down_mid = lax.optimization_barrier((left, right, up_mid, down_mid))
    sides = jnp.concatenate([left, right], axis=3)
    up_sides = shifted(sides, "height", True)
    down_sides = shifted(sides, "height", False)
    row = jnp.concatenate([left, kv_blocks, right], axis=3)
    up = jnp.concatenate([up_sides[:, :, :, :1], up_mid, up_sides[:, :, :, 1:]], axis=3)
    down = jnp.concatenate([down_sides[:, :, :, :1], down_mid, down_sides[:, :, :, 1:]], axis=3)
    return jnp.concatenate([up, row, down], axis=2)


PACK = 128


def attention_kernel(listed_ref, q_ref, *refs):
    nlist = (len(refs) - 2) // 2
    key_refs, value_refs = refs[:nlist], refs[nlist : 2 * nlist]
    keep_ref, out_ref = refs[2 * nlist], refs[2 * nlist + 1]
    rows = q_ref.shape[0]
    frames = key_refs[0].shape[1]
    keep = keep_ref[...] > 0
    lane = lax.broadcasted_iota(jnp.int32, (1, 2 * HD), 1)
    low = lane < HD
    stat_lane = lax.broadcasted_iota(jnp.int32, (1, PACK), 1)
    stats = jnp.zeros((rows, PACK), jnp.float32)
    scale = jnp.asarray(1.0 / 8.0, jnp.bfloat16)
    blocks = []
    for pair in range(HEADS // 2):
        cols = pl.ds(pair * 2 * HD, 2 * HD)
        q2 = q_ref[:, cols] * scale
        k2 = jnp.concatenate(
            [r[0, f, 0, :, cols] for r in key_refs for f in range(frames)], axis=0
        )
        v2 = jnp.concatenate(
            [r[0, f, 0, :, cols] for r in value_refs for f in range(frames)], axis=0
        )
        outs = []
        for part in range(2):
            mine = low if part == 0 else jnp.logical_not(low)
            qh = jnp.where(mine, q2, jnp.zeros_like(q2))
            scores = lax.dot_general(
                qh, k2, (((1,), (1,)), ((), ())), preferred_element_type=jnp.float32
            )
            scores = jnp.where(keep, scores, jnp.float32(-1e30))
            top = jnp.max(scores, axis=1, keepdims=True)
            probs = jnp.exp(scores - top)
            total = jnp.sum(probs, axis=1, keepdims=True)
            outs.append(
                jnp.dot(probs.astype(jnp.bfloat16), v2, preferred_element_type=jnp.float32)
            )
            head = pair * 2 + part
            stats = jnp.where(stat_lane == head, top, stats)
            stats = jnp.where(stat_lane == HEADS + head, total, stats)
        blocks.append(jnp.where(low, outs[0], outs[1]))
    out_ref[...] = jnp.concatenate(blocks + [stats], axis=1)


def attention(query_rows, hood, listed, keep):
    qtok, width = query_rows.shape
    _, frames, _, blk, _ = hood.shape
    nlist = listed.shape[0]
    count = nlist * frames * blk
    tiles = qtok // TQ
    flops = 2 * 2 * qtok * count * 2 * width
    block = (1, frames, 1, blk, width)

    def entry_spec(kind, e):
        return pl.BlockSpec(block, lambda i, lst: (kind, 0, lst[e], 0, 0))

    grid_spec = pltpu.PrefetchScalarGridSpec(
        num_scalar_prefetch=1,
        grid=(tiles,),
        in_specs=[pl.BlockSpec((TQ, width), lambda i, lst: (i, 0))]
        + [entry_spec(0, e) for e in range(nlist)]
        + [entry_spec(1, e) for e in range(nlist)]
        + [pl.BlockSpec((1, count), lambda i, lst: (0, 0))],
        out_specs=pl.BlockSpec((TQ, width + PACK), lambda i, lst: (i, 0)),
    )
    return pl.pallas_call(
        attention_kernel,
        grid_spec=grid_spec,
        out_shape=jax.ShapeDtypeStruct((qtok, width + PACK), jnp.float32),
        cost_estimate=pl.CostEstimate(
            flops=flops,
            transcendentals=qtok * count * HEADS,
            bytes_accessed=qtok * width * 6 + count * width * 4,
        ),
    )(listed, query_rows, *([hood] * (2 * nlist)), keep)


def merge_kernel(a_ref, b_ref, *out_refs):
    width = a_ref.shape[1] - PACK
    sa = a_ref[:, pl.ds(width, PACK)]
    sb = b_ref[:, pl.ds(width, PACK)]
    stat_lane = lax.broadcasted_iota(jnp.int32, (1, PACK), 1)
    top = jnp.maximum(sa, sb)
    fa = jnp.exp(sa - top)
    fb = jnp.exp(sb - top)
    heads_a = [jnp.sum(jnp.where(stat_lane == h, fa, 0.0), axis=1, keepdims=True) for h in range(HEADS)]
    heads_b = [jnp.sum(jnp.where(stat_lane == h, fb, 0.0), axis=1, keepdims=True) for h in range(HEADS)]
    spread_a = jnp.zeros_like(sa)
    spread_b = jnp.zeros_like(sb)
    for h in range(HEADS):
        spread_a = jnp.where(stat_lane == HEADS + h, heads_a[h], spread_a)
        spread_b = jnp.where(stat_lane == HEADS + h, heads_b[h], spread_b)
    tot = sa * spread_a + sb * spread_b
    stats = jnp.where(
        stat_lane < HEADS, top, jnp.where(stat_lane < 2 * HEADS, tot, jnp.float32(0.0))
    )
    lane = lax.broadcasted_iota(jnp.int32, (1, 2 * HD), 1)
    low = lane < HD
    blocks = []
    for pair in range(HEADS // 2):
        cols = pl.ds(pair * 2 * HD, 2 * HD)
        f_a = jnp.where(low, heads_a[2 * pair], heads_a[2 * pair + 1])
        f_b = jnp.where(low, heads_b[2 * pair], heads_b[2 * pair + 1])
        blocks.append(a_ref[:, cols] * f_a + b_ref[:, cols] * f_b)
    merged = jnp.concatenate(blocks + [stats], axis=1)
    if len(out_refs) == 1:
        out_refs[0][...] = merged
    else:
        half = merged.shape[0] // 2
        out_refs[0][...] = merged[:half]
        out_refs[1][...] = merged[half:]


def merge(kept, got, split):
    rows, cols = kept.shape
    count = 2 if split else 1
    shape = jax.ShapeDtypeStruct((rows // count, cols), jnp.float32)
    return pl.pallas_call(
        merge_kernel,
        out_shape=[shape] * count,
        cost_estimate=pl.CostEstimate(
            flops=4 * rows * cols, transcendentals=2 * rows * PACK, bytes_accessed=12 * rows * cols
        ),
    )(kept, got)


def step_bits(nbits, core):
    if nbits != 5:
        return [jnp.int32(b) for b in range(nbits)]
    first, second = [0, 1, 3, 2, 4], [0, 3, 1, 4, 2]
    return [jnp.where(core == 0, a, b) for a, b in zip(first, second)]


def step_pairs(nbits, step):
    pairs = []
    for t in range(1 << nbits):
        bits = [0, 1, 3, 2, 4] if t % 2 == 0 else [0, 3, 1, 4, 2]
        bit = bits[step] if nbits == 5 else step
        pairs.append((t, t ^ (1 << bit)))
    return pairs


def block_order(groups, me):
    nbits = groups.bit_length() - 1
    order = step_bits(nbits, me & 1)
    pos = jnp.arange(groups, dtype=jnp.int32)
    block = jnp.zeros_like(pos)
    for i, bit in enumerate(order):
        a = (pos >> (nbits - 1 - i)) & 1
        block = block + ((a ^ ((me >> bit) & 1)) << bit)
    return block


def tree_reduce(first, second):
    groups = lax.axis_size("tm")
    nbits = groups.bit_length() - 1
    for i in range(nbits):
        got = lax.ppermute(second, "tm", step_pairs(nbits, i))
        last = i == nbits - 1
        outs = merge(first, got, not last)
        if last:
            return outs[0]
        first, second = outs


def local(queries, kv_blocks, block_list, block_valid, w_out):
    hood = neighbourhood(kv_blocks)
    frames = hood.shape[1]
    nblk = hood.shape[4]
    blk = hood.shape[5]
    width = hood.shape[6]
    hood = hood.reshape(2, frames, 9 * nblk, blk, width)
    listed = block_list[0, 0]
    nlist = listed.shape[0]
    keep = jnp.broadcast_to((block_valid[0, 0] > 0)[:, None, None], (nlist, frames, blk))
    keep = keep.reshape(1, -1).astype(jnp.int32)
    query_rows = queries[0, 0]
    qtok = query_rows.shape[0]
    groups = lax.axis_size("tm")
    me = lax.axis_index("tm")
    order = jnp.concatenate(
        [block_order(groups, me)[: groups // 2], block_order(groups, me ^ 1)[: groups // 2]]
    )
    query_rows = jnp.take(query_rows.reshape(groups, qtok // groups, width), order, axis=0)
    query_rows = query_rows.reshape(qtok, width)
    second = attention(query_rows[qtok // 2 :], hood, listed, keep)
    first = attention(query_rows[: qtok // 2], hood, listed, keep)
    final = tree_reduce(first, second)
    summed = final[:, :width]
    total = final[:, width + HEADS : width + 2 * HEADS]
    own_rows = summed.shape[0]
    attended = summed / jnp.repeat(total, HD, axis=1)
    normed = attended * lax.rsqrt(jnp.mean(attended * attended, axis=1, keepdims=True) + 1e-06)
    normed = normed.astype(jnp.bfloat16)
    joined = jnp.dot(normed, w_out, preferred_element_type=jnp.float32)
    return joined.reshape(1, 1, own_rows, width)


def solution(mesh):
    in_specs = (
        P("height", "width", None, None),
        P(None, "tm", "height", "width", None, None, None),
        P("height", "width", None),
        P("height", "width", None),
        P(),
    )
    out_specs = P("height", "width", "tm", None)
    return jax.shard_map(local, mesh=mesh, in_specs=in_specs, out_specs=out_specs, check_vma=False)
```

```python
import jax
import jax.numpy as jnp
from jax import lax
from jax.experimental import pallas as pl
from jax.experimental.pallas import tpu as pltpu
from jax.sharding import PartitionSpec as P

HEADS = 8
HD = 64
TQ = 512


def shifted(array, axis, forward):
    size = lax.axis_size(axis)
    if forward:
        pairs = [(i, i + 1) for i in range(size - 1)]
    else:
        pairs = [(i + 1, i) for i in range(size - 1)]
    return lax.ppermute(array, axis, pairs)


def neighbourhood(kv_blocks):
    left = shifted(kv_blocks, "width", True)
    right = shifted(kv_blocks, "width", False)
    up_mid = shifted(kv_blocks, "height", True)
    down_mid = shifted(kv_blocks, "height", False)
    left, right, up_mid, down_mid = lax.optimization_barrier((left, right, up_mid, down_mid))
    sides = jnp.concatenate([left, right], axis=3)
    up_sides = shifted(sides, "height", True)
    down_sides = shifted(sides, "height", False)
    row = jnp.concatenate([left, kv_blocks, right], axis=3)
    up = jnp.concatenate([up_sides[:, :, :, :1], up_mid, up_sides[:, :, :, 1:]], axis=3)
    down = jnp.concatenate([down_sides[:, :, :, :1], down_mid, down_sides[:, :, :, 1:]], axis=3)
    return jnp.concatenate([up, row, down], axis=2)


PACK = 128


def attention_kernel(listed_ref, q_ref, *refs):
    nlist = (len(refs) - 2) // 2
    key_refs, value_refs = refs[:nlist], refs[nlist : 2 * nlist]
    keep_ref, out_ref = refs[2 * nlist], refs[2 * nlist + 1]
    rows = q_ref.shape[0]
    frames = key_refs[0].shape[1]
    keep = keep_ref[...] > 0
    lane = lax.broadcasted_iota(jnp.int32, (1, 2 * HD), 1)
    low = lane < HD
    stat_lane = lax.broadcasted_iota(jnp.int32, (1, PACK), 1)
    stats = jnp.zeros((rows, PACK), jnp.float32)
    scale = jnp.asarray(1.0 / 8.0, jnp.bfloat16)
    blocks = []
    for pair in range(HEADS // 2):
        cols = pl.ds(pair * 2 * HD, 2 * HD)
        q2 = q_ref[:, cols] * scale
        k2 = jnp.concatenate(
            [r[0, f, 0, :, cols] for r in key_refs for f in range(frames)], axis=0
        )
        v2 = jnp.concatenate(
            [r[0, f, 0, :, cols] for r in value_refs for f in range(frames)], axis=0
        )
        outs = []
        for part in range(2):
            mine = low if part == 0 else jnp.logical_not(low)
            qh = jnp.where(mine, q2, jnp.zeros_like(q2))
            scores = lax.dot_general(
                qh, k2, (((1,), (1,)), ((), ())), preferred_element_type=jnp.float32
            )
            scores = jnp.where(keep, scores, jnp.float32(-1e30))
            top = jnp.max(scores, axis=1, keepdims=True)
            probs = jnp.exp(scores - top)
            total = jnp.sum(probs, axis=1, keepdims=True)
            outs.append(
                jnp.dot(probs.astype(jnp.bfloat16), v2, preferred_element_type=jnp.float32)
            )
            head = pair * 2 + part
            stats = jnp.where(stat_lane == head, top, stats)
            stats = jnp.where(stat_lane == HEADS + head, total, stats)
        blocks.append(jnp.where(low, outs[0], outs[1]))
    out_ref[...] = jnp.concatenate(blocks + [stats], axis=1)


def attention(query_rows, hood, listed, keep):
    qtok, width = query_rows.shape
    _, frames, _, blk, _ = hood.shape
    nlist = listed.shape[0]
    count = nlist * frames * blk
    tiles = qtok // TQ
    flops = 2 * 2 * qtok * count * 2 * width
    block = (1, frames, 1, blk, width)

    def entry_spec(kind, e):
        return pl.BlockSpec(block, lambda i, lst: (kind, 0, lst[e], 0, 0))

    grid_spec = pltpu.PrefetchScalarGridSpec(
        num_scalar_prefetch=1,
        grid=(tiles,),
        in_specs=[pl.BlockSpec((TQ, width), lambda i, lst: (i, 0))]
        + [entry_spec(0, e) for e in range(nlist)]
        + [entry_spec(1, e) for e in range(nlist)]
        + [pl.BlockSpec((1, count), lambda i, lst: (0, 0))],
        out_specs=pl.BlockSpec((TQ, width + PACK), lambda i, lst: (i, 0)),
    )
    return pl.pallas_call(
        attention_kernel,
        grid_spec=grid_spec,
        out_shape=jax.ShapeDtypeStruct((qtok, width + PACK), jnp.float32),
        cost_estimate=pl.CostEstimate(
            flops=flops,
            transcendentals=qtok * count * HEADS,
            bytes_accessed=qtok * width * 6 + count * width * 4,
        ),
    )(listed, query_rows, *([hood] * (2 * nlist)), keep)


def merge_kernel(a_ref, b_ref, *out_refs):
    width = a_ref.shape[1] - PACK
    sa = a_ref[:, pl.ds(width, PACK)]
    sb = b_ref[:, pl.ds(width, PACK)]
    stat_lane = lax.broadcasted_iota(jnp.int32, (1, PACK), 1)
    top = jnp.maximum(sa, sb)
    fa = jnp.exp(sa - top)
    fb = jnp.exp(sb - top)
    heads_a = [jnp.sum(jnp.where(stat_lane == h, fa, 0.0), axis=1, keepdims=True) for h in range(HEADS)]
    heads_b = [jnp.sum(jnp.where(stat_lane == h, fb, 0.0), axis=1, keepdims=True) for h in range(HEADS)]
    spread_a = jnp.zeros_like(sa)
    spread_b = jnp.zeros_like(sb)
    for h in range(HEADS):
        spread_a = jnp.where(stat_lane == HEADS + h, heads_a[h], spread_a)
        spread_b = jnp.where(stat_lane == HEADS + h, heads_b[h], spread_b)
    tot = sa * spread_a + sb * spread_b
    stats = jnp.where(
        stat_lane < HEADS, top, jnp.where(stat_lane < 2 * HEADS, tot, jnp.float32(0.0))
    )
    lane = lax.broadcasted_iota(jnp.int32, (1, 2 * HD), 1)
    low = lane < HD
    blocks = []
    for pair in range(HEADS // 2):
        cols = pl.ds(pair * 2 * HD, 2 * HD)
        f_a = jnp.where(low, heads_a[2 * pair], heads_a[2 * pair + 1])
        f_b = jnp.where(low, heads_b[2 * pair], heads_b[2 * pair + 1])
        blocks.append(a_ref[:, cols] * f_a + b_ref[:, cols] * f_b)
    merged = jnp.concatenate(blocks + [stats], axis=1)
    if len(out_refs) == 1:
        out_refs[0][...] = merged
    else:
        half = merged.shape[0] // 2
        out_refs[0][...] = merged[:half]
        out_refs[1][...] = merged[half:]


def merge(kept, got, split):
    rows, cols = kept.shape
    count = 2 if split else 1
    shape = jax.ShapeDtypeStruct((rows // count, cols), jnp.float32)
    return pl.pallas_call(
        merge_kernel,
        out_shape=[shape] * count,
        cost_estimate=pl.CostEstimate(
            flops=4 * rows * cols, transcendentals=2 * rows * PACK, bytes_accessed=12 * rows * cols
        ),
    )(kept, got)


def step_bits(nbits, core):
    if nbits != 5:
        return [jnp.int32(b) for b in range(nbits)]
    first, second = [0, 1, 3, 2, 4], [0, 3, 1, 4, 2]
    return [jnp.where(core == 0, a, b) for a, b in zip(first, second)]


def step_pairs(nbits, step):
    pairs = []
    for t in range(1 << nbits):
        bits = [0, 1, 3, 2, 4] if t % 2 == 0 else [0, 3, 1, 4, 2]
        bit = bits[step] if nbits == 5 else step
        pairs.append((t, t ^ (1 << bit)))
    return pairs


def block_order(groups, me):
    nbits = groups.bit_length() - 1
    order = step_bits(nbits, me & 1)
    pos = jnp.arange(groups, dtype=jnp.int32)
    block = jnp.zeros_like(pos)
    for i, bit in enumerate(order):
        a = (pos >> (nbits - 1 - i)) & 1
        block = block + ((a ^ ((me >> bit) & 1)) << bit)
    return block


def tree_reduce(first, second):
    groups = lax.axis_size("tm")
    nbits = groups.bit_length() - 1
    for i in range(nbits):
        got = lax.ppermute(second, "tm", step_pairs(nbits, i))
        last = i == nbits - 1
        outs = merge(first, got, not last)
        if last:
            return outs[0]
        first, second = outs


def local(queries, kv_blocks, block_list, block_valid, w_out):
    hood = neighbourhood(kv_blocks)
    frames = hood.shape[1]
    nblk = hood.shape[4]
    blk = hood.shape[5]
    width = hood.shape[6]
    hood = hood.reshape(2, frames, 9 * nblk, blk, width)
    listed = block_list[0, 0]
    nlist = listed.shape[0]
    keep = jnp.broadcast_to((block_valid[0, 0] > 0)[:, None, None], (nlist, frames, blk))
    keep = keep.reshape(1, -1).astype(jnp.int32)
    query_rows = queries[0, 0]
    qtok = query_rows.shape[0]
    groups = lax.axis_size("tm")
    me = lax.axis_index("tm")
    order = jnp.concatenate(
        [block_order(groups, me)[: groups // 2], block_order(groups, me ^ 1)[: groups // 2]]
    )
    query_rows = jnp.take(query_rows.reshape(groups, qtok // groups, width), order, axis=0)
    query_rows = query_rows.reshape(qtok, width)
    second = attention(query_rows[qtok // 2 :], hood, listed, keep)
    first = attention(query_rows[: qtok // 2], hood, listed, keep)
    final = tree_reduce(first, second)
    summed = final[:, :width]
    total = final[:, width + HEADS : width + 2 * HEADS]
    own_rows = summed.shape[0]
    attended = summed / jnp.repeat(total, HD, axis=1)
    normed = attended * lax.rsqrt(jnp.mean(attended * attended, axis=1, keepdims=True) + 1e-06)
    normed = normed.astype(jnp.bfloat16)
    joined = jnp.dot(normed, w_out, preferred_element_type=jnp.float32)
    return joined.reshape(1, 1, own_rows, width)


def solution(mesh):
    in_specs = (
        P("height", "width", None, None),
        P(None, "tm", "height", "width", None, None, None),
        P("height", "width", None),
        P("height", "width", None),
        P(),
    )
    out_specs = P("height", "width", "tm", None)
    return jax.shard_map(local, mesh=mesh, in_specs=in_specs, out_specs=out_specs, check_vma=False)
```

```python
import jax
import jax.numpy as jnp
from jax import lax
from jax.experimental import pallas as pl
from jax.experimental.pallas import tpu as pltpu
from jax.sharding import PartitionSpec as P

HEADS = 8
HD = 64
TQ = 512


def shifted(array, axis, forward):
    size = lax.axis_size(axis)
    if forward:
        pairs = [(i, i + 1) for i in range(size - 1)]
    else:
        pairs = [(i + 1, i) for i in range(size - 1)]
    return lax.ppermute(array, axis, pairs)


def neighbourhood(kv_blocks):
    left = shifted(kv_blocks, "width", True)
    right = shifted(kv_blocks, "width", False)
    up_mid = shifted(kv_blocks, "height", True)
    down_mid = shifted(kv_blocks, "height", False)
    left, right, up_mid, down_mid = lax.optimization_barrier((left, right, up_mid, down_mid))
    sides = jnp.concatenate([left, right], axis=3)
    up_sides = shifted(sides, "height", True)
    down_sides = shifted(sides, "height", False)
    row = jnp.concatenate([left, kv_blocks, right], axis=3)
    up = jnp.concatenate([up_sides[:, :, :, :1], up_mid, up_sides[:, :, :, 1:]], axis=3)
    down = jnp.concatenate([down_sides[:, :, :, :1], down_mid, down_sides[:, :, :, 1:]], axis=3)
    return jnp.concatenate([up, row, down], axis=2)


PACK = 128


def attention_kernel(listed_ref, q_ref, *refs):
    nlist = (len(refs) - 2) // 2
    key_refs, value_refs = refs[:nlist], refs[nlist : 2 * nlist]
    keep_ref, out_ref = refs[2 * nlist], refs[2 * nlist + 1]
    rows = q_ref.shape[0]
    frames = key_refs[0].shape[1]
    keep = keep_ref[...] > 0
    lane = lax.broadcasted_iota(jnp.int32, (1, 2 * HD), 1)
    low = lane < HD
    stat_lane = lax.broadcasted_iota(jnp.int32, (1, PACK), 1)
    stats = jnp.zeros((rows, PACK), jnp.float32)
    scale = jnp.asarray(1.0 / 8.0, jnp.bfloat16)
    blocks = []
    for pair in range(HEADS // 2):
        cols = pl.ds(pair * 2 * HD, 2 * HD)
        q2 = q_ref[:, cols] * scale
        k2 = jnp.concatenate(
            [r[0, f, 0, :, cols] for r in key_refs for f in range(frames)], axis=0
        )
        v2 = jnp.concatenate(
            [r[0, f, 0, :, cols] for r in value_refs for f in range(frames)], axis=0
        )
        outs = []
        for part in range(2):
            mine = low if part == 0 else jnp.logical_not(low)
            qh = jnp.where(mine, q2, jnp.zeros_like(q2))
            scores = lax.dot_general(
                qh, k2, (((1,), (1,)), ((), ())), preferred_element_type=jnp.float32
            )
            scores = jnp.where(keep, scores, jnp.float32(-1e30))
            top = jnp.max(scores, axis=1, keepdims=True)
            probs = jnp.exp(scores - top)
            total = jnp.sum(probs, axis=1, keepdims=True)
            outs.append(
                jnp.dot(probs.astype(jnp.bfloat16), v2, preferred_element_type=jnp.float32)
            )
            head = pair * 2 + part
            stats = jnp.where(stat_lane == head, top, stats)
            stats = jnp.where(stat_lane == HEADS + head, total, stats)
        blocks.append(jnp.where(low, outs[0], outs[1]))
    out_ref[...] = jnp.concatenate(blocks + [stats], axis=1)


def attention(query_rows, hood, listed, keep):
    qtok, width = query_rows.shape
    _, frames, _, blk, _ = hood.shape
    nlist = listed.shape[0]
    count = nlist * frames * blk
    tq = min(TQ, qtok)
    tiles = qtok // tq
    flops = 2 * 2 * qtok * count * 2 * width
    block = (1, frames, 1, blk, width)

    def entry_spec(kind, e):
        return pl.BlockSpec(block, lambda i, lst: (kind, 0, lst[e], 0, 0))

    grid_spec = pltpu.PrefetchScalarGridSpec(
        num_scalar_prefetch=1,
        grid=(tiles,),
        in_specs=[pl.BlockSpec((tq, width), lambda i, lst: (i, 0))]
        + [entry_spec(0, e) for e in range(nlist)]
        + [entry_spec(1, e) for e in range(nlist)]
        + [pl.BlockSpec((1, count), lambda i, lst: (0, 0))],
        out_specs=pl.BlockSpec((tq, width + PACK), lambda i, lst: (i, 0)),
    )
    return pl.pallas_call(
        attention_kernel,
        grid_spec=grid_spec,
        out_shape=jax.ShapeDtypeStruct((qtok, width + PACK), jnp.float32),
        cost_estimate=pl.CostEstimate(
            flops=flops,
            transcendentals=qtok * count * HEADS,
            bytes_accessed=qtok * width * 6 + count * width * 4,
        ),
    )(listed, query_rows, *([hood] * (2 * nlist)), keep)


def merge_kernel(a_ref, b_ref, *out_refs):
    width = a_ref.shape[1] - PACK
    sa = a_ref[:, pl.ds(width, PACK)]
    sb = b_ref[:, pl.ds(width, PACK)]
    stat_lane = lax.broadcasted_iota(jnp.int32, (1, PACK), 1)
    top = jnp.maximum(sa, sb)
    fa = jnp.exp(sa - top)
    fb = jnp.exp(sb - top)
    heads_a = [jnp.sum(jnp.where(stat_lane == h, fa, 0.0), axis=1, keepdims=True) for h in range(HEADS)]
    heads_b = [jnp.sum(jnp.where(stat_lane == h, fb, 0.0), axis=1, keepdims=True) for h in range(HEADS)]
    spread_a = jnp.zeros_like(sa)
    spread_b = jnp.zeros_like(sb)
    for h in range(HEADS):
        spread_a = jnp.where(stat_lane == HEADS + h, heads_a[h], spread_a)
        spread_b = jnp.where(stat_lane == HEADS + h, heads_b[h], spread_b)
    tot = sa * spread_a + sb * spread_b
    stats = jnp.where(
        stat_lane < HEADS, top, jnp.where(stat_lane < 2 * HEADS, tot, jnp.float32(0.0))
    )
    lane = lax.broadcasted_iota(jnp.int32, (1, 2 * HD), 1)
    low = lane < HD
    blocks = []
    for pair in range(HEADS // 2):
        cols = pl.ds(pair * 2 * HD, 2 * HD)
        f_a = jnp.where(low, heads_a[2 * pair], heads_a[2 * pair + 1])
        f_b = jnp.where(low, heads_b[2 * pair], heads_b[2 * pair + 1])
        blocks.append(a_ref[:, cols] * f_a + b_ref[:, cols] * f_b)
    merged = jnp.concatenate(blocks + [stats], axis=1)
    if len(out_refs) == 1:
        out_refs[0][...] = merged
    else:
        half = merged.shape[0] // 2
        out_refs[0][...] = merged[:half]
        out_refs[1][...] = merged[half:]


def merge(kept, got, split, offset=0):
    rows, cols = kept.shape
    count = 2 if split else 1
    shape = jax.ShapeDtypeStruct((rows // count, cols), jnp.float32)
    if split:
        out_specs = [pl.BlockSpec((rows // 2, cols), lambda i: (0, 0))] * 2
    else:
        out_specs = [pl.BlockSpec((rows, cols), lambda i: (0, 0))]
    return pl.pallas_call(
        merge_kernel,
        grid=(1,),
        in_specs=[
            pl.BlockSpec((rows, cols), lambda i: (0, 0)),
            pl.BlockSpec((rows, cols), lambda i: (offset // rows, 0)),
        ],
        out_specs=out_specs,
        out_shape=[shape] * count,
        cost_estimate=pl.CostEstimate(
            flops=4 * rows * cols, transcendentals=2 * rows * PACK, bytes_accessed=12 * rows * cols
        ),
    )(kept, got)


def step_bits(nbits, core):
    if nbits != 5:
        return [jnp.int32(b) for b in range(nbits)]
    first, second = [0, 1, 3, 2, 4], [0, 3, 1, 4, 2]
    return [jnp.where(core == 0, a, b) for a, b in zip(first, second)]


def step_pairs(nbits, step):
    pairs = []
    for t in range(1 << nbits):
        bits = [0, 1, 3, 2, 4] if t % 2 == 0 else [0, 3, 1, 4, 2]
        bit = bits[step] if nbits == 5 else step
        pairs.append((t, t ^ (1 << bit)))
    return pairs


def block_order(groups, me):
    nbits = groups.bit_length() - 1
    order = step_bits(nbits, me & 1)
    pos = jnp.arange(groups, dtype=jnp.int32)
    block = jnp.zeros_like(pos)
    for i, bit in enumerate(order):
        a = (pos >> (nbits - 1 - i)) & 1
        block = block + ((a ^ ((me >> bit) & 1)) << bit)
    return block


def tree_reduce(query_rows, hood, listed, keep):
    groups = lax.axis_size("tm")
    nbits = groups.bit_length() - 1
    qtok = query_rows.shape[0]
    half, quarter = qtok // 2, qtok // 4
    second = attention(query_rows[half:], hood, listed, keep)
    got_first = lax.ppermute(second, "tm", step_pairs(nbits, 0))
    sent = attention(query_rows[quarter:half], hood, listed, keep)
    (sent,) = merge(sent, got_first, False, quarter)
    second = lax.ppermute(sent, "tm", step_pairs(nbits, 1))
    first = attention(query_rows[:quarter], hood, listed, keep)
    (first,) = merge(first, got_first, False, 0)
    for i in range(1, nbits):
        last = i == nbits - 1
        outs = merge(first, second, not last)
        if last:
            return outs[0]
        first, second = outs
        second = lax.ppermute(second, "tm", step_pairs(nbits, i + 1))


def local(queries, kv_blocks, block_list, block_valid, w_out):
    hood = neighbourhood(kv_blocks)
    frames = hood.shape[1]
    nblk = hood.shape[4]
    blk = hood.shape[5]
    width = hood.shape[6]
    hood = hood.reshape(2, frames, 9 * nblk, blk, width)
    listed = block_list[0, 0]
    nlist = listed.shape[0]
    keep = jnp.broadcast_to((block_valid[0, 0] > 0)[:, None, None], (nlist, frames, blk))
    keep = keep.reshape(1, -1).astype(jnp.int32)
    query_rows = queries[0, 0]
    qtok = query_rows.shape[0]
    groups = lax.axis_size("tm")
    me = lax.axis_index("tm")
    order = jnp.concatenate(
        [block_order(groups, me)[: groups // 2], block_order(groups, me ^ 1)[: groups // 2]]
    )
    query_rows = jnp.take(query_rows.reshape(groups, qtok // groups, width), order, axis=0)
    query_rows = query_rows.reshape(qtok, width)
    final = tree_reduce(query_rows, hood, listed, keep)
    summed = final[:, :width]
    total = final[:, width + HEADS : width + 2 * HEADS]
    own_rows = summed.shape[0]
    attended = summed / jnp.repeat(total, HD, axis=1)
    normed = attended * lax.rsqrt(jnp.mean(attended * attended, axis=1, keepdims=True) + 1e-06)
    normed = normed.astype(jnp.bfloat16)
    joined = jnp.dot(normed, w_out, preferred_element_type=jnp.float32)
    return joined.reshape(1, 1, own_rows, width)


def solution(mesh):
    in_specs = (
        P("height", "width", None, None),
        P(None, "tm", "height", "width", None, None, None),
        P("height", "width", None),
        P("height", "width", None),
        P(),
    )
    out_specs = P("height", "width", "tm", None)
    return jax.shard_map(local, mesh=mesh, in_specs=in_specs, out_specs=out_specs, check_vma=False)
```

```python
import jax
import jax.numpy as jnp
from jax import lax
from jax.experimental import pallas as pl
from jax.experimental.pallas import tpu as pltpu
from jax.sharding import PartitionSpec as P

HEADS = 8
HD = 64
TQ = 512


def shifted(array, axis, forward):
    size = lax.axis_size(axis)
    if forward:
        pairs = [(i, i + 1) for i in range(size - 1)]
    else:
        pairs = [(i + 1, i) for i in range(size - 1)]
    return lax.ppermute(array, axis, pairs)


def neighbourhood(kv_blocks):
    left = shifted(kv_blocks, "width", True)
    right = shifted(kv_blocks, "width", False)
    up_mid = shifted(kv_blocks, "height", True)
    down_mid = shifted(kv_blocks, "height", False)
    left, right, up_mid, down_mid = lax.optimization_barrier((left, right, up_mid, down_mid))
    sides = jnp.concatenate([left, right], axis=3)
    up_sides = shifted(sides, "height", True)
    down_sides = shifted(sides, "height", False)
    row = jnp.concatenate([left, kv_blocks, right], axis=3)
    up = jnp.concatenate([up_sides[:, :, :, :1], up_mid, up_sides[:, :, :, 1:]], axis=3)
    down = jnp.concatenate([down_sides[:, :, :, :1], down_mid, down_sides[:, :, :, 1:]], axis=3)
    return jnp.concatenate([up, row, down], axis=2)


PACK = 128


def attention_kernel(listed_ref, q_ref, *refs):
    nlist = (len(refs) - 2) // 2
    key_refs, value_refs = refs[:nlist], refs[nlist : 2 * nlist]
    keep_ref, out_ref = refs[2 * nlist], refs[2 * nlist + 1]
    rows = q_ref.shape[0]
    frames = key_refs[0].shape[1]
    keep = keep_ref[...] > 0
    lane = lax.broadcasted_iota(jnp.int32, (1, 2 * HD), 1)
    low = lane < HD
    stat_lane = lax.broadcasted_iota(jnp.int32, (1, PACK), 1)
    stats = jnp.zeros((rows, PACK), jnp.float32)
    scale = jnp.asarray(1.0 / 8.0, jnp.bfloat16)
    blocks = []
    for pair in range(HEADS // 2):
        cols = pl.ds(pair * 2 * HD, 2 * HD)
        q2 = q_ref[:, cols] * scale
        k2 = jnp.concatenate(
            [r[0, f, 0, :, cols] for r in key_refs for f in range(frames)], axis=0
        )
        v2 = jnp.concatenate(
            [r[0, f, 0, :, cols] for r in value_refs for f in range(frames)], axis=0
        )
        outs = []
        for part in range(2):
            mine = low if part == 0 else jnp.logical_not(low)
            qh = jnp.where(mine, q2, jnp.zeros_like(q2))
            scores = lax.dot_general(
                qh, k2, (((1,), (1,)), ((), ())), preferred_element_type=jnp.float32
            )
            scores = jnp.where(keep, scores, jnp.float32(-1e30))
            top = jnp.max(scores, axis=1, keepdims=True)
            probs = jnp.exp(scores - top)
            total = jnp.sum(probs, axis=1, keepdims=True)
            outs.append(
                jnp.dot(probs.astype(jnp.bfloat16), v2, preferred_element_type=jnp.float32)
            )
            head = pair * 2 + part
            stats = jnp.where(stat_lane == head, top, stats)
            stats = jnp.where(stat_lane == HEADS + head, total, stats)
        blocks.append(jnp.where(low, outs[0], outs[1]))
    out_ref[...] = jnp.concatenate(blocks + [stats], axis=1)


def attention(query_rows, hood, listed, keep):
    qtok, width = query_rows.shape
    _, frames, _, blk, _ = hood.shape
    nlist = listed.shape[0]
    count = nlist * frames * blk
    tq = min(TQ, qtok)
    tiles = qtok // tq
    flops = 2 * 2 * qtok * count * 2 * width
    block = (1, frames, 1, blk, width)

    def entry_spec(kind, e):
        return pl.BlockSpec(block, lambda i, lst: (kind, 0, lst[e], 0, 0))

    grid_spec = pltpu.PrefetchScalarGridSpec(
        num_scalar_prefetch=1,
        grid=(tiles,),
        in_specs=[pl.BlockSpec((tq, width), lambda i, lst: (i, 0))]
        + [entry_spec(0, e) for e in range(nlist)]
        + [entry_spec(1, e) for e in range(nlist)]
        + [pl.BlockSpec((1, count), lambda i, lst: (0, 0))],
        out_specs=pl.BlockSpec((tq, width + PACK), lambda i, lst: (i, 0)),
    )
    return pl.pallas_call(
        attention_kernel,
        grid_spec=grid_spec,
        out_shape=jax.ShapeDtypeStruct((qtok, width + PACK), jnp.float32),
        cost_estimate=pl.CostEstimate(
            flops=flops,
            transcendentals=qtok * count * HEADS,
            bytes_accessed=qtok * width * 6 + count * width * 4,
        ),
    )(listed, query_rows, *([hood] * (2 * nlist)), keep)


def merge_kernel(a_ref, b_ref, *out_refs):
    width = a_ref.shape[1] - PACK
    sa = a_ref[:, pl.ds(width, PACK)]
    sb = b_ref[:, pl.ds(width, PACK)]
    stat_lane = lax.broadcasted_iota(jnp.int32, (1, PACK), 1)
    top = jnp.maximum(sa, sb)
    fa = jnp.exp(sa - top)
    fb = jnp.exp(sb - top)
    heads_a = [jnp.sum(jnp.where(stat_lane == h, fa, 0.0), axis=1, keepdims=True) for h in range(HEADS)]
    heads_b = [jnp.sum(jnp.where(stat_lane == h, fb, 0.0), axis=1, keepdims=True) for h in range(HEADS)]
    spread_a = jnp.zeros_like(sa)
    spread_b = jnp.zeros_like(sb)
    for h in range(HEADS):
        spread_a = jnp.where(stat_lane == HEADS + h, heads_a[h], spread_a)
        spread_b = jnp.where(stat_lane == HEADS + h, heads_b[h], spread_b)
    tot = sa * spread_a + sb * spread_b
    stats = jnp.where(
        stat_lane < HEADS, top, jnp.where(stat_lane < 2 * HEADS, tot, jnp.float32(0.0))
    )
    lane = lax.broadcasted_iota(jnp.int32, (1, 2 * HD), 1)
    low = lane < HD
    blocks = []
    for pair in range(HEADS // 2):
        cols = pl.ds(pair * 2 * HD, 2 * HD)
        f_a = jnp.where(low, heads_a[2 * pair], heads_a[2 * pair + 1])
        f_b = jnp.where(low, heads_b[2 * pair], heads_b[2 * pair + 1])
        blocks.append(a_ref[:, cols] * f_a + b_ref[:, cols] * f_b)
    merged = jnp.concatenate(blocks + [stats], axis=1)
    if len(out_refs) == 1:
        out_refs[0][...] = merged
    else:
        half = merged.shape[0] // 2
        out_refs[0][...] = merged[:half]
        out_refs[1][...] = merged[half:]


def merge(kept, got, split, offset=0):
    rows, cols = kept.shape
    count = 2 if split else 1
    shape = jax.ShapeDtypeStruct((rows // count, cols), jnp.float32)
    if split:
        out_specs = [pl.BlockSpec((rows // 2, cols), lambda i: (0, 0))] * 2
    else:
        out_specs = [pl.BlockSpec((rows, cols), lambda i: (0, 0))]
    return pl.pallas_call(
        merge_kernel,
        grid=(1,),
        in_specs=[
            pl.BlockSpec((rows, cols), lambda i: (0, 0)),
            pl.BlockSpec((rows, cols), lambda i: (offset // rows, 0)),
        ],
        out_specs=out_specs,
        out_shape=[shape] * count,
        cost_estimate=pl.CostEstimate(
            flops=4 * rows * cols, transcendentals=2 * rows * PACK, bytes_accessed=12 * rows * cols
        ),
    )(kept, got)


def step_bits(nbits, core):
    if nbits != 5:
        return [jnp.int32(b) for b in range(nbits)]
    first, second = [0, 1, 3, 2, 4], [0, 3, 1, 4, 2]
    return [jnp.where(core == 0, a, b) for a, b in zip(first, second)]


def step_pairs(nbits, step):
    pairs = []
    for t in range(1 << nbits):
        bits = [0, 1, 3, 2, 4] if t % 2 == 0 else [0, 3, 1, 4, 2]
        bit = bits[step] if nbits == 5 else step
        pairs.append((t, t ^ (1 << bit)))
    return pairs


def block_order(groups, me):
    nbits = groups.bit_length() - 1
    order = step_bits(nbits, me & 1)
    pos = jnp.arange(groups, dtype=jnp.int32)
    block = jnp.zeros_like(pos)
    for i, bit in enumerate(order):
        a = (pos >> (nbits - 1 - i)) & 1
        block = block + ((a ^ ((me >> bit) & 1)) << bit)
    return block


def tree_reduce(query_rows, hood, listed, keep):
    groups = lax.axis_size("tm")
    nbits = groups.bit_length() - 1
    qtok = query_rows.shape[0]
    half, quarter, eighth = qtok // 2, qtok // 4, qtok // 8
    second = attention(query_rows[half:], hood, listed, keep)
    got_1 = lax.ppermute(second, "tm", step_pairs(nbits, 0))
    sent = attention(query_rows[quarter:half], hood, listed, keep)
    (sent,) = merge(sent, got_1, False, quarter)
    got_2 = lax.ppermute(sent, "tm", step_pairs(nbits, 1))
    sent = attention(query_rows[eighth:quarter], hood, listed, keep)
    (sent,) = merge(sent, got_1, False, eighth)
    (sent,) = merge(sent, got_2, False, eighth)
    second = lax.ppermute(sent, "tm", step_pairs(nbits, 2))
    first = attention(query_rows[:eighth], hood, listed, keep)
    (first,) = merge(first, got_1, False, 0)
    (first,) = merge(first, got_2, False, 0)
    for i in range(2, nbits):
        last = i == nbits - 1
        outs = merge(first, second, not last)
        if last:
            return outs[0]
        first, second = outs
        second = lax.ppermute(second, "tm", step_pairs(nbits, i + 1))


def local(queries, kv_blocks, block_list, block_valid, w_out):
    hood = neighbourhood(kv_blocks)
    frames = hood.shape[1]
    nblk = hood.shape[4]
    blk = hood.shape[5]
    width = hood.shape[6]
    hood = hood.reshape(2, frames, 9 * nblk, blk, width)
    listed = block_list[0, 0]
    nlist = listed.shape[0]
    keep = jnp.broadcast_to((block_valid[0, 0] > 0)[:, None, None], (nlist, frames, blk))
    keep = keep.reshape(1, -1).astype(jnp.int32)
    query_rows = queries[0, 0]
    qtok = query_rows.shape[0]
    groups = lax.axis_size("tm")
    me = lax.axis_index("tm")
    order = jnp.concatenate(
        [block_order(groups, me)[: groups // 2], block_order(groups, me ^ 1)[: groups // 2]]
    )
    query_rows = jnp.take(query_rows.reshape(groups, qtok // groups, width), order, axis=0)
    query_rows = query_rows.reshape(qtok, width)
    final = tree_reduce(query_rows, hood, listed, keep)
    summed = final[:, :width]
    total = final[:, width + HEADS : width + 2 * HEADS]
    own_rows = summed.shape[0]
    attended = summed / jnp.repeat(total, HD, axis=1)
    normed = attended * lax.rsqrt(jnp.mean(attended * attended, axis=1, keepdims=True) + 1e-06)
    normed = normed.astype(jnp.bfloat16)
    joined = jnp.dot(normed, w_out, preferred_element_type=jnp.float32)
    return joined.reshape(1, 1, own_rows, width)


def solution(mesh):
    in_specs = (
        P("height", "width", None, None),
        P(None, "tm", "height", "width", None, None, None),
        P("height", "width", None),
        P("height", "width", None),
        P(),
    )
    out_specs = P("height", "width", "tm", None)
    return jax.shard_map(local, mesh=mesh, in_specs=in_specs, out_specs=out_specs, check_vma=False)
```

```python
import jax
import jax.numpy as jnp
from jax import lax
from jax.experimental import pallas as pl
from jax.experimental.pallas import tpu as pltpu
from jax.sharding import PartitionSpec as P

HEADS = 8
HD = 64
TQ = 512


def shifted(array, axis, forward):
    size = lax.axis_size(axis)
    if forward:
        pairs = [(i, i + 1) for i in range(size - 1)]
    else:
        pairs = [(i + 1, i) for i in range(size - 1)]
    return lax.ppermute(array, axis, pairs)


def neighbourhood(kv_blocks):
    left = shifted(kv_blocks, "width", True)
    right = shifted(kv_blocks, "width", False)
    up_mid = shifted(kv_blocks, "height", True)
    down_mid = shifted(kv_blocks, "height", False)
    left, right, up_mid, down_mid = lax.optimization_barrier((left, right, up_mid, down_mid))
    sides = jnp.concatenate([left, right], axis=3)
    up_sides = shifted(sides, "height", True)
    down_sides = shifted(sides, "height", False)
    row = jnp.concatenate([left, kv_blocks, right], axis=3)
    up = jnp.concatenate([up_sides[:, :, :, :1], up_mid, up_sides[:, :, :, 1:]], axis=3)
    down = jnp.concatenate([down_sides[:, :, :, :1], down_mid, down_sides[:, :, :, 1:]], axis=3)
    return jnp.concatenate([up, row, down], axis=2)


PACK = 128


def attention_kernel(listed_ref, q_ref, *refs):
    nlist = (len(refs) - 2) // 2
    key_refs, value_refs = refs[:nlist], refs[nlist : 2 * nlist]
    keep_ref, out_ref = refs[2 * nlist], refs[2 * nlist + 1]
    rows = q_ref.shape[0]
    frames = key_refs[0].shape[1]
    keep = keep_ref[...] > 0
    lane = lax.broadcasted_iota(jnp.int32, (1, 2 * HD), 1)
    low = lane < HD
    stat_lane = lax.broadcasted_iota(jnp.int32, (1, PACK), 1)
    stats = jnp.zeros((rows, PACK), jnp.float32)
    scale = jnp.asarray(1.0 / 8.0, jnp.bfloat16)
    blocks = []
    for pair in range(HEADS // 2):
        cols = pl.ds(pair * 2 * HD, 2 * HD)
        q2 = q_ref[:, cols] * scale
        k2 = jnp.concatenate(
            [r[0, f, 0, :, cols] for r in key_refs for f in range(frames)], axis=0
        )
        v2 = jnp.concatenate(
            [r[0, f, 0, :, cols] for r in value_refs for f in range(frames)], axis=0
        )
        outs = []
        for part in range(2):
            mine = low if part == 0 else jnp.logical_not(low)
            qh = jnp.where(mine, q2, jnp.zeros_like(q2))
            scores = lax.dot_general(
                qh, k2, (((1,), (1,)), ((), ())), preferred_element_type=jnp.float32
            )
            scores = jnp.where(keep, scores, jnp.float32(-1e30))
            top = jnp.max(scores, axis=1, keepdims=True)
            probs = jnp.exp(scores - top)
            total = jnp.sum(probs, axis=1, keepdims=True)
            outs.append(
                jnp.dot(probs.astype(jnp.bfloat16), v2, preferred_element_type=jnp.float32)
            )
            head = pair * 2 + part
            stats = jnp.where(stat_lane == head, top, stats)
            stats = jnp.where(stat_lane == HEADS + head, total, stats)
        blocks.append(jnp.where(low, outs[0], outs[1]))
    out_ref[...] = jnp.concatenate(blocks + [stats], axis=1)


def attention(query_rows, hood, listed, keep):
    qtok, width = query_rows.shape
    _, frames, _, blk, _ = hood.shape
    nlist = listed.shape[0]
    count = nlist * frames * blk
    tq = min(TQ, qtok)
    tiles = qtok // tq
    flops = 2 * 2 * qtok * count * 2 * width
    block = (1, frames, 1, blk, width)

    def entry_spec(kind, e):
        return pl.BlockSpec(block, lambda i, lst: (kind, 0, lst[e], 0, 0))

    grid_spec = pltpu.PrefetchScalarGridSpec(
        num_scalar_prefetch=1,
        grid=(tiles,),
        in_specs=[pl.BlockSpec((tq, width), lambda i, lst: (i, 0))]
        + [entry_spec(0, e) for e in range(nlist)]
        + [entry_spec(1, e) for e in range(nlist)]
        + [pl.BlockSpec((1, count), lambda i, lst: (0, 0))],
        out_specs=pl.BlockSpec((tq, width + PACK), lambda i, lst: (i, 0)),
    )
    return pl.pallas_call(
        attention_kernel,
        grid_spec=grid_spec,
        out_shape=jax.ShapeDtypeStruct((qtok, width + PACK), jnp.float32),
        cost_estimate=pl.CostEstimate(
            flops=flops,
            transcendentals=qtok * count * HEADS,
            bytes_accessed=qtok * width * 6 + count * width * 4,
        ),
    )(listed, query_rows, *([hood] * (2 * nlist)), keep)


def merge_kernel(a_ref, b_ref, *out_refs):
    width = a_ref.shape[1] - PACK
    sa = a_ref[:, pl.ds(width, PACK)]
    sb = b_ref[:, pl.ds(width, PACK)]
    stat_lane = lax.broadcasted_iota(jnp.int32, (1, PACK), 1)
    top = jnp.maximum(sa, sb)
    fa = jnp.exp(sa - top)
    fb = jnp.exp(sb - top)
    heads_a = [jnp.sum(jnp.where(stat_lane == h, fa, 0.0), axis=1, keepdims=True) for h in range(HEADS)]
    heads_b = [jnp.sum(jnp.where(stat_lane == h, fb, 0.0), axis=1, keepdims=True) for h in range(HEADS)]
    spread_a = jnp.zeros_like(sa)
    spread_b = jnp.zeros_like(sb)
    for h in range(HEADS):
        spread_a = jnp.where(stat_lane == HEADS + h, heads_a[h], spread_a)
        spread_b = jnp.where(stat_lane == HEADS + h, heads_b[h], spread_b)
    tot = sa * spread_a + sb * spread_b
    stats = jnp.where(
        stat_lane < HEADS, top, jnp.where(stat_lane < 2 * HEADS, tot, jnp.float32(0.0))
    )
    lane = lax.broadcasted_iota(jnp.int32, (1, 2 * HD), 1)
    low = lane < HD
    blocks = []
    for pair in range(HEADS // 2):
        cols = pl.ds(pair * 2 * HD, 2 * HD)
        f_a = jnp.where(low, heads_a[2 * pair], heads_a[2 * pair + 1])
        f_b = jnp.where(low, heads_b[2 * pair], heads_b[2 * pair + 1])
        blocks.append(a_ref[:, cols] * f_a + b_ref[:, cols] * f_b)
    merged = jnp.concatenate(blocks + [stats], axis=1)
    if len(out_refs) == 1:
        out_refs[0][...] = merged
    else:
        half = merged.shape[0] // 2
        out_refs[0][...] = merged[:half]
        out_refs[1][...] = merged[half:]


def merge(kept, got, split, offset=0):
    rows, cols = kept.shape
    count = 2 if split else 1
    shape = jax.ShapeDtypeStruct((rows // count, cols), jnp.float32)
    if split:
        out_specs = [pl.BlockSpec((rows // 2, cols), lambda i: (0, 0))] * 2
    else:
        out_specs = [pl.BlockSpec((rows, cols), lambda i: (0, 0))]
    return pl.pallas_call(
        merge_kernel,
        grid=(1,),
        in_specs=[
            pl.BlockSpec((rows, cols), lambda i: (0, 0)),
            pl.BlockSpec((rows, cols), lambda i: (offset // rows, 0)),
        ],
        out_specs=out_specs,
        out_shape=[shape] * count,
        cost_estimate=pl.CostEstimate(
            flops=4 * rows * cols, transcendentals=2 * rows * PACK, bytes_accessed=12 * rows * cols
        ),
    )(kept, got)


def finish_kernel(a_ref, b_ref, w_ref, out_ref):
    tmp = a_ref.shape
    merge_kernel(a_ref, b_ref, _Sink(tmp))
    merged = _Sink.value
    width = tmp[1] - PACK
    stats = merged[:, width:]
    stat_lane = lax.broadcasted_iota(jnp.int32, (1, PACK), 1)
    totals = [
        jnp.sum(jnp.where(stat_lane == HEADS + h, stats, 0.0), axis=1, keepdims=True)
        for h in range(HEADS)
    ]
    lane = lax.broadcasted_iota(jnp.int32, (1, 2 * HD), 1)
    low = lane < HD
    blocks = []
    for pair in range(HEADS // 2):
        block = merged[:, pair * 2 * HD : (pair + 1) * 2 * HD]
        blocks.append(block / jnp.where(low, totals[2 * pair], totals[2 * pair + 1]))
    attended = jnp.concatenate(blocks, axis=1)
    square = jnp.mean(attended * attended, axis=1, keepdims=True)
    normed = (attended * lax.rsqrt(square + 1e-06)).astype(jnp.bfloat16)
    out_ref[...] = jnp.dot(normed, w_ref[...], preferred_element_type=jnp.float32)


class _Sink:
    value = None

    def __init__(self, shape):
        self.shape = shape

    def __setitem__(self, index, value):
        _Sink.value = value


def finish(kept, got, w_out):
    rows, cols = kept.shape
    width = w_out.shape[1]
    return pl.pallas_call(
        finish_kernel,
        out_shape=jax.ShapeDtypeStruct((rows, width), jnp.float32),
        cost_estimate=pl.CostEstimate(
            flops=2 * rows * cols * width, transcendentals=rows, bytes_accessed=2 * cols * width
        ),
    )(kept, got, w_out)


def step_bits(nbits, core):
    if nbits != 5:
        return [jnp.int32(b) for b in range(nbits)]
    first, second = [0, 1, 3, 2, 4], [0, 3, 1, 4, 2]
    return [jnp.where(core == 0, a, b) for a, b in zip(first, second)]


def step_pairs(nbits, step):
    pairs = []
    for t in range(1 << nbits):
        bits = [0, 1, 3, 2, 4] if t % 2 == 0 else [0, 3, 1, 4, 2]
        bit = bits[step] if nbits == 5 else step
        pairs.append((t, t ^ (1 << bit)))
    return pairs


def block_order(groups, me):
    nbits = groups.bit_length() - 1
    order = step_bits(nbits, me & 1)
    pos = jnp.arange(groups, dtype=jnp.int32)
    block = jnp.zeros_like(pos)
    for i, bit in enumerate(order):
        a = (pos >> (nbits - 1 - i)) & 1
        block = block + ((a ^ ((me >> bit) & 1)) << bit)
    return block


def tree_reduce(query_rows, hood, listed, keep, w_out):
    groups = lax.axis_size("tm")
    nbits = groups.bit_length() - 1
    qtok = query_rows.shape[0]
    half, quarter = qtok // 2, qtok // 4
    second = attention(query_rows[half:], hood, listed, keep)
    got_first = lax.ppermute(second, "tm", step_pairs(nbits, 0))
    sent = attention(query_rows[quarter:half], hood, listed, keep)
    (sent,) = merge(sent, got_first, False, quarter)
    second = lax.ppermute(sent, "tm", step_pairs(nbits, 1))
    first = attention(query_rows[:quarter], hood, listed, keep)
    (first,) = merge(first, got_first, False, 0)
    for i in range(1, nbits):
        if i == nbits - 1:
            return finish(first, second, w_out)
        outs = merge(first, second, True)
        first, second = outs
        second = lax.ppermute(second, "tm", step_pairs(nbits, i + 1))


def local(queries, kv_blocks, block_list, block_valid, w_out):
    hood = neighbourhood(kv_blocks)
    frames = hood.shape[1]
    nblk = hood.shape[4]
    blk = hood.shape[5]
    width = hood.shape[6]
    hood = hood.reshape(2, frames, 9 * nblk, blk, width)
    listed = block_list[0, 0]
    nlist = listed.shape[0]
    keep = jnp.broadcast_to((block_valid[0, 0] > 0)[:, None, None], (nlist, frames, blk))
    keep = keep.reshape(1, -1).astype(jnp.int32)
    query_rows = queries[0, 0]
    qtok = query_rows.shape[0]
    groups = lax.axis_size("tm")
    me = lax.axis_index("tm")
    order = jnp.concatenate(
        [block_order(groups, me)[: groups // 2], block_order(groups, me ^ 1)[: groups // 2]]
    )
    query_rows = jnp.take(query_rows.reshape(groups, qtok // groups, width), order, axis=0)
    query_rows = query_rows.reshape(qtok, width)
    joined = tree_reduce(query_rows, hood, listed, keep, w_out)
    return joined.reshape(1, 1, joined.shape[0], width)


def solution(mesh):
    in_specs = (
        P("height", "width", None, None),
        P(None, "tm", "height", "width", None, None, None),
        P("height", "width", None),
        P("height", "width", None),
        P(),
    )
    out_specs = P("height", "width", "tm", None)
    return jax.shard_map(local, mesh=mesh, in_specs=in_specs, out_specs=out_specs, check_vma=False)
```

```python
import functools

import jax
import jax.numpy as jnp
from jax import lax
from jax.experimental import pallas as pl
from jax.experimental.pallas import tpu as pltpu
from jax.sharding import PartitionSpec as P

HEADS = 8
HD = 64
TQ = 512


def shifted(array, axis, forward):
    size = lax.axis_size(axis)
    if forward:
        pairs = [(i, i + 1) for i in range(size - 1)]
    else:
        pairs = [(i + 1, i) for i in range(size - 1)]
    return lax.ppermute(array, axis, pairs)


def neighbourhood(kv_blocks):
    left = shifted(kv_blocks, "width", True)
    right = shifted(kv_blocks, "width", False)
    up_mid = shifted(kv_blocks, "height", True)
    down_mid = shifted(kv_blocks, "height", False)
    left, right, up_mid, down_mid = lax.optimization_barrier((left, right, up_mid, down_mid))
    sides = jnp.concatenate([left, right], axis=3)
    up_sides = shifted(sides, "height", True)
    down_sides = shifted(sides, "height", False)
    row = jnp.concatenate([left, kv_blocks, right], axis=3)
    up = jnp.concatenate([up_sides[:, :, :, :1], up_mid, up_sides[:, :, :, 1:]], axis=3)
    down = jnp.concatenate([down_sides[:, :, :, :1], down_mid, down_sides[:, :, :, 1:]], axis=3)
    return jnp.concatenate([up, row, down], axis=2)


PACK = 128


def attention_kernel(gather, *refs):
    if gather:
        listed_ref, q_ref = refs[0], refs[1]
        refs = refs[2:]
        nlist = (len(refs) - 4) // 2
        key_refs, value_refs = refs[:nlist], refs[nlist : 2 * nlist]
        keep_ref, out_ref, keys_out, values_out = refs[2 * nlist :]
        frames = key_refs[0].shape[1]
    else:
        q_ref, keys_ref, values_ref, keep_ref, out_ref = refs
    rows = q_ref.shape[0]
    keep = keep_ref[...] > 0
    lane = lax.broadcasted_iota(jnp.int32, (1, 2 * HD), 1)
    low = lane < HD
    stat_lane = lax.broadcasted_iota(jnp.int32, (1, PACK), 1)
    stats = jnp.zeros((rows, PACK), jnp.float32)
    scale = jnp.asarray(1.0 / 8.0, jnp.bfloat16)
    blocks = []
    for pair in range(HEADS // 2):
        cols = pl.ds(pair * 2 * HD, 2 * HD)
        q2 = q_ref[:, cols] * scale
        if gather:
            k2 = jnp.concatenate(
                [r[0, f, 0, :, cols] for r in key_refs for f in range(frames)], axis=0
            )
            v2 = jnp.concatenate(
                [r[0, f, 0, :, cols] for r in value_refs for f in range(frames)], axis=0
            )
            keys_out[:, cols] = k2
            values_out[:, cols] = v2
        else:
            k2 = keys_ref[:, cols]
            v2 = values_ref[:, cols]
        outs = []
        for part in range(2):
            mine = low if part == 0 else jnp.logical_not(low)
            qh = jnp.where(mine, q2, jnp.zeros_like(q2))
            scores = lax.dot_general(
                qh, k2, (((1,), (1,)), ((), ())), preferred_element_type=jnp.float32
            )
            scores = jnp.where(keep, scores, jnp.float32(-1e30))
            top = jnp.max(scores, axis=1, keepdims=True)
            probs = jnp.exp(scores - top)
            total = jnp.sum(probs, axis=1, keepdims=True)
            outs.append(
                jnp.dot(probs.astype(jnp.bfloat16), v2, preferred_element_type=jnp.float32)
            )
            head = pair * 2 + part
            stats = jnp.where(stat_lane == head, top, stats)
            stats = jnp.where(stat_lane == HEADS + head, total, stats)
        blocks.append(jnp.where(low, outs[0], outs[1]))
    out_ref[...] = jnp.concatenate(blocks + [stats], axis=1)


def attention(query_rows, hood, listed, keep):
    qtok, width = query_rows.shape
    _, frames, _, blk, _ = hood.shape
    nlist = listed.shape[0]
    count = nlist * frames * blk
    flops = 2 * 2 * qtok * count * 2 * width
    block = (1, frames, 1, blk, width)

    def entry_spec(kind, e):
        return pl.BlockSpec(block, lambda i, lst: (kind, 0, lst[e], 0, 0))

    whole = pl.BlockSpec((count, width), lambda i, lst: (0, 0))
    grid_spec = pltpu.PrefetchScalarGridSpec(
        num_scalar_prefetch=1,
        grid=(1,),
        in_specs=[pl.BlockSpec((qtok, width), lambda i, lst: (0, 0))]
        + [entry_spec(0, e) for e in range(nlist)]
        + [entry_spec(1, e) for e in range(nlist)]
        + [pl.BlockSpec((1, count), lambda i, lst: (0, 0))],
        out_specs=[pl.BlockSpec((qtok, width + PACK), lambda i, lst: (0, 0)), whole, whole],
    )
    return pl.pallas_call(
        functools.partial(attention_kernel, True),
        grid_spec=grid_spec,
        out_shape=[
            jax.ShapeDtypeStruct((qtok, width + PACK), jnp.float32),
            jax.ShapeDtypeStruct((count, width), hood.dtype),
            jax.ShapeDtypeStruct((count, width), hood.dtype),
        ],
        cost_estimate=pl.CostEstimate(
            flops=flops,
            transcendentals=qtok * count * HEADS,
            bytes_accessed=qtok * width * 6 + count * width * 8,
        ),
    )(listed, query_rows, *([hood] * (2 * nlist)), keep)


def attention_again(query_rows, keys, values, keep):
    qtok, width = query_rows.shape
    count = keys.shape[0]
    flops = 2 * 2 * qtok * count * 2 * width
    return pl.pallas_call(
        functools.partial(attention_kernel, False),
        out_shape=jax.ShapeDtypeStruct((qtok, width + PACK), jnp.float32),
        cost_estimate=pl.CostEstimate(
            flops=flops,
            transcendentals=qtok * count * HEADS,
            bytes_accessed=qtok * width * 6 + count * width * 4,
        ),
    )(query_rows, keys, values, keep)


def merge_kernel(a_ref, b_ref, *out_refs):
    width = a_ref.shape[1] - PACK
    sa = a_ref[:, pl.ds(width, PACK)]
    sb = b_ref[:, pl.ds(width, PACK)]
    stat_lane = lax.broadcasted_iota(jnp.int32, (1, PACK), 1)
    top = jnp.maximum(sa, sb)
    fa = jnp.exp(sa - top)
    fb = jnp.exp(sb - top)
    heads_a = [jnp.sum(jnp.where(stat_lane == h, fa, 0.0), axis=1, keepdims=True) for h in range(HEADS)]
    heads_b = [jnp.sum(jnp.where(stat_lane == h, fb, 0.0), axis=1, keepdims=True) for h in range(HEADS)]
    spread_a = jnp.zeros_like(sa)
    spread_b = jnp.zeros_like(sb)
    for h in range(HEADS):
        spread_a = jnp.where(stat_lane == HEADS + h, heads_a[h], spread_a)
        spread_b = jnp.where(stat_lane == HEADS + h, heads_b[h], spread_b)
    tot = sa * spread_a + sb * spread_b
    stats = jnp.where(
        stat_lane < HEADS, top, jnp.where(stat_lane < 2 * HEADS, tot, jnp.float32(0.0))
    )
    lane = lax.broadcasted_iota(jnp.int32, (1, 2 * HD), 1)
    low = lane < HD
    blocks = []
    for pair in range(HEADS // 2):
        cols = pl.ds(pair * 2 * HD, 2 * HD)
        f_a = jnp.where(low, heads_a[2 * pair], heads_a[2 * pair + 1])
        f_b = jnp.where(low, heads_b[2 * pair], heads_b[2 * pair + 1])
        blocks.append(a_ref[:, cols] * f_a + b_ref[:, cols] * f_b)
    merged = jnp.concatenate(blocks + [stats], axis=1)
    if len(out_refs) == 1:
        out_refs[0][...] = merged
    else:
        half = merged.shape[0] // 2
        out_refs[0][...] = merged[:half]
        out_refs[1][...] = merged[half:]


def merge(kept, got, split, offset=0):
    rows, cols = kept.shape
    count = 2 if split else 1
    shape = jax.ShapeDtypeStruct((rows // count, cols), jnp.float32)
    if split:
        out_specs = [pl.BlockSpec((rows // 2, cols), lambda i: (0, 0))] * 2
    else:
        out_specs = [pl.BlockSpec((rows, cols), lambda i: (0, 0))]
    return pl.pallas_call(
        merge_kernel,
        grid=(1,),
        in_specs=[
            pl.BlockSpec((rows, cols), lambda i: (0, 0)),
            pl.BlockSpec((rows, cols), lambda i: (offset // rows, 0)),
        ],
        out_specs=out_specs,
        out_shape=[shape] * count,
        cost_estimate=pl.CostEstimate(
            flops=4 * rows * cols, transcendentals=2 * rows * PACK, bytes_accessed=12 * rows * cols
        ),
    )(kept, got)


def finish_kernel(a_ref, b_ref, w_ref, out_ref):
    tmp = a_ref.shape
    merge_kernel(a_ref, b_ref, _Sink(tmp))
    merged = _Sink.value
    width = tmp[1] - PACK
    stats = merged[:, width:]
    stat_lane = lax.broadcasted_iota(jnp.int32, (1, PACK), 1)
    totals = [
        jnp.sum(jnp.where(stat_lane == HEADS + h, stats, 0.0), axis=1, keepdims=True)
        for h in range(HEADS)
    ]
    lane = lax.broadcasted_iota(jnp.int32, (1, 2 * HD), 1)
    low = lane < HD
    blocks = []
    for pair in range(HEADS // 2):
        block = merged[:, pair * 2 * HD : (pair + 1) * 2 * HD]
        blocks.append(block / jnp.where(low, totals[2 * pair], totals[2 * pair + 1]))
    attended = jnp.concatenate(blocks, axis=1)
    square = jnp.mean(attended * attended, axis=1, keepdims=True)
    normed = (attended * lax.rsqrt(square + 1e-06)).astype(jnp.bfloat16)
    out_ref[...] = jnp.dot(normed, w_ref[...], preferred_element_type=jnp.float32)


class _Sink:
    value = None

    def __init__(self, shape):
        self.shape = shape

    def __setitem__(self, index, value):
        _Sink.value = value


def finish(kept, got, w_out):
    rows, cols = kept.shape
    width = w_out.shape[1]
    return pl.pallas_call(
        finish_kernel,
        out_shape=jax.ShapeDtypeStruct((rows, width), jnp.float32),
        cost_estimate=pl.CostEstimate(
            flops=2 * rows * cols * width, transcendentals=rows, bytes_accessed=2 * cols * width
        ),
    )(kept, got, w_out)


def step_bits(nbits, core):
    if nbits != 5:
        return [jnp.int32(b) for b in range(nbits)]
    first, second = [0, 1, 3, 2, 4], [0, 3, 1, 4, 2]
    return [jnp.where(core == 0, a, b) for a, b in zip(first, second)]


def step_pairs(nbits, step):
    pairs = []
    for t in range(1 << nbits):
        bits = [0, 1, 3, 2, 4] if t % 2 == 0 else [0, 3, 1, 4, 2]
        bit = bits[step] if nbits == 5 else step
        pairs.append((t, t ^ (1 << bit)))
    return pairs


def block_order(groups, me):
    nbits = groups.bit_length() - 1
    order = step_bits(nbits, me & 1)
    pos = jnp.arange(groups, dtype=jnp.int32)
    block = jnp.zeros_like(pos)
    for i, bit in enumerate(order):
        a = (pos >> (nbits - 1 - i)) & 1
        block = block + ((a ^ ((me >> bit) & 1)) << bit)
    return block


def tree_reduce(query_rows, hood, listed, keep, w_out):
    groups = lax.axis_size("tm")
    nbits = groups.bit_length() - 1
    qtok = query_rows.shape[0]
    half, quarter = qtok // 2, qtok // 4
    second, keys, values = attention(query_rows[half:], hood, listed, keep)
    got_first = lax.ppermute(second, "tm", step_pairs(nbits, 0))
    sent = attention_again(query_rows[quarter:half], keys, values, keep)
    (sent,) = merge(sent, got_first, False, quarter)
    second = lax.ppermute(sent, "tm", step_pairs(nbits, 1))
    first = attention_again(query_rows[:quarter], keys, values, keep)
    (first,) = merge(first, got_first, False, 0)
    for i in range(1, nbits):
        if i == nbits - 1:
            return finish(first, second, w_out)
        outs = merge(first, second, True)
        first, second = outs
        second = lax.ppermute(second, "tm", step_pairs(nbits, i + 1))


def local(queries, kv_blocks, block_list, block_valid, w_out):
    hood = neighbourhood(kv_blocks)
    frames = hood.shape[1]
    nblk = hood.shape[4]
    blk = hood.shape[5]
    width = hood.shape[6]
    hood = hood.reshape(2, frames, 9 * nblk, blk, width)
    listed = block_list[0, 0]
    nlist = listed.shape[0]
    keep = jnp.broadcast_to((block_valid[0, 0] > 0)[:, None, None], (nlist, frames, blk))
    keep = keep.reshape(1, -1).astype(jnp.int32)
    query_rows = queries[0, 0]
    qtok = query_rows.shape[0]
    groups = lax.axis_size("tm")
    me = lax.axis_index("tm")
    order = jnp.concatenate(
        [block_order(groups, me)[: groups // 2], block_order(groups, me ^ 1)[: groups // 2]]
    )
    query_rows = jnp.take(query_rows.reshape(groups, qtok // groups, width), order, axis=0)
    query_rows = query_rows.reshape(qtok, width)
    joined = tree_reduce(query_rows, hood, listed, keep, w_out)
    return joined.reshape(1, 1, joined.shape[0], width)


def solution(mesh):
    in_specs = (
        P("height", "width", None, None),
        P(None, "tm", "height", "width", None, None, None),
        P("height", "width", None),
        P("height", "width", None),
        P(),
    )
    out_specs = P("height", "width", "tm", None)
    return jax.shard_map(local, mesh=mesh, in_specs=in_specs, out_specs=out_specs, check_vma=False)
```

```python
import jax
import jax.numpy as jnp
from jax import lax
from jax.experimental import pallas as pl
from jax.experimental.pallas import tpu as pltpu
from jax.sharding import PartitionSpec as P

HEADS = 8
HD = 64
TQ = 512


def shifted(array, axis, forward):
    size = lax.axis_size(axis)
    if forward:
        pairs = [(i, i + 1) for i in range(size - 1)]
    else:
        pairs = [(i + 1, i) for i in range(size - 1)]
    return lax.ppermute(array, axis, pairs)


def neighbourhood(kv_blocks):
    left = shifted(kv_blocks, "width", True)
    right = shifted(kv_blocks, "width", False)
    up_mid = shifted(kv_blocks, "height", True)
    down_mid = shifted(kv_blocks, "height", False)
    left, right, up_mid, down_mid = lax.optimization_barrier((left, right, up_mid, down_mid))
    sides = jnp.concatenate([left, right], axis=3)
    up_sides = shifted(sides, "height", True)
    down_sides = shifted(sides, "height", False)
    row = jnp.concatenate([left, kv_blocks, right], axis=3)
    up = jnp.concatenate([up_sides[:, :, :, :1], up_mid, up_sides[:, :, :, 1:]], axis=3)
    down = jnp.concatenate([down_sides[:, :, :, :1], down_mid, down_sides[:, :, :, 1:]], axis=3)
    return jnp.concatenate([up, row, down], axis=2)


PACK = 128


def attention_kernel(listed_ref, q_ref, *refs):
    nlist = (len(refs) - 2) // 2
    key_refs, value_refs = refs[:nlist], refs[nlist : 2 * nlist]
    keep_ref, out_ref = refs[2 * nlist], refs[2 * nlist + 1]
    rows = q_ref.shape[0]
    frames = key_refs[0].shape[1]
    keep = keep_ref[...] > 0
    lane = lax.broadcasted_iota(jnp.int32, (1, 2 * HD), 1)
    low = lane < HD
    stat_lane = lax.broadcasted_iota(jnp.int32, (1, PACK), 1)
    stats = jnp.zeros((rows, PACK), jnp.float32)
    scale = jnp.asarray(1.0 / 8.0, jnp.bfloat16)
    blocks = []
    for pair in range(HEADS // 2):
        cols = pl.ds(pair * 2 * HD, 2 * HD)
        q2 = q_ref[:, cols] * scale
        k2 = jnp.concatenate(
            [r[0, f, 0, :, cols] for r in key_refs for f in range(frames)], axis=0
        )
        v2 = jnp.concatenate(
            [r[0, f, 0, :, cols] for r in value_refs for f in range(frames)], axis=0
        )
        outs = []
        for part in range(2):
            mine = low if part == 0 else jnp.logical_not(low)
            qh = jnp.where(mine, q2, jnp.zeros_like(q2))
            scores = lax.dot_general(
                qh, k2, (((1,), (1,)), ((), ())), preferred_element_type=jnp.float32
            )
            scores = jnp.where(keep, scores, jnp.float32(-1e30))
            top = jnp.max(scores, axis=1, keepdims=True)
            probs = jnp.exp(scores - top)
            total = jnp.sum(probs, axis=1, keepdims=True)
            outs.append(
                jnp.dot(probs.astype(jnp.bfloat16), v2, preferred_element_type=jnp.float32)
            )
            head = pair * 2 + part
            stats = jnp.where(stat_lane == head, top, stats)
            stats = jnp.where(stat_lane == HEADS + head, total, stats)
        blocks.append(jnp.where(low, outs[0], outs[1]))
    out_ref[...] = jnp.concatenate(blocks + [stats], axis=1)


def attention(query_rows, hood, listed, keep):
    qtok, width = query_rows.shape
    _, frames, _, blk, _ = hood.shape
    nlist = listed.shape[0]
    count = nlist * frames * blk
    tq = min(TQ, qtok)
    tiles = qtok // tq
    flops = 2 * 2 * qtok * count * 2 * width
    block = (1, frames, 1, blk, width)

    def entry_spec(kind, e):
        return pl.BlockSpec(block, lambda i, lst: (kind, 0, lst[e], 0, 0))

    grid_spec = pltpu.PrefetchScalarGridSpec(
        num_scalar_prefetch=1,
        grid=(tiles,),
        in_specs=[pl.BlockSpec((tq, width), lambda i, lst: (i, 0))]
        + [entry_spec(0, e) for e in range(nlist)]
        + [entry_spec(1, e) for e in range(nlist)]
        + [pl.BlockSpec((1, count), lambda i, lst: (0, 0))],
        out_specs=pl.BlockSpec((tq, width + PACK), lambda i, lst: (i, 0)),
    )
    return pl.pallas_call(
        attention_kernel,
        grid_spec=grid_spec,
        out_shape=jax.ShapeDtypeStruct((qtok, width + PACK), jnp.float32),
        cost_estimate=pl.CostEstimate(
            flops=flops,
            transcendentals=qtok * count * HEADS,
            bytes_accessed=qtok * width * 6 + count * width * 4,
        ),
    )(listed, query_rows, *([hood] * (2 * nlist)), keep)


def merge_kernel(a_ref, b_ref, *out_refs):
    width = a_ref.shape[1] - PACK
    sa = a_ref[:, pl.ds(width, PACK)]
    sb = b_ref[:, pl.ds(width, PACK)]
    stat_lane = lax.broadcasted_iota(jnp.int32, (1, PACK), 1)
    top = jnp.maximum(sa, sb)
    fa = jnp.exp(sa - top)
    fb = jnp.exp(sb - top)
    heads_a = [jnp.sum(jnp.where(stat_lane == h, fa, 0.0), axis=1, keepdims=True) for h in range(HEADS)]
    heads_b = [jnp.sum(jnp.where(stat_lane == h, fb, 0.0), axis=1, keepdims=True) for h in range(HEADS)]
    spread_a = jnp.zeros_like(sa)
    spread_b = jnp.zeros_like(sb)
    for h in range(HEADS):
        spread_a = jnp.where(stat_lane == HEADS + h, heads_a[h], spread_a)
        spread_b = jnp.where(stat_lane == HEADS + h, heads_b[h], spread_b)
    tot = sa * spread_a + sb * spread_b
    stats = jnp.where(
        stat_lane < HEADS, top, jnp.where(stat_lane < 2 * HEADS, tot, jnp.float32(0.0))
    )
    lane = lax.broadcasted_iota(jnp.int32, (1, 2 * HD), 1)
    low = lane < HD
    blocks = []
    for pair in range(HEADS // 2):
        cols = pl.ds(pair * 2 * HD, 2 * HD)
        f_a = jnp.where(low, heads_a[2 * pair], heads_a[2 * pair + 1])
        f_b = jnp.where(low, heads_b[2 * pair], heads_b[2 * pair + 1])
        blocks.append(a_ref[:, cols] * f_a + b_ref[:, cols] * f_b)
    merged = jnp.concatenate(blocks + [stats], axis=1)
    if len(out_refs) == 1:
        out_refs[0][...] = merged
    else:
        half = merged.shape[0] // 2
        out_refs[0][...] = merged[:half]
        out_refs[1][...] = merged[half:]


def merge_part(kept, got, start, rows):
    cols = kept.shape[1]
    spec = pl.BlockSpec((rows, cols), lambda i: (start // rows, 0))
    return pl.pallas_call(
        merge_kernel,
        grid=(1,),
        in_specs=[spec, spec],
        out_specs=[pl.BlockSpec((rows, cols), lambda i: (0, 0))],
        out_shape=[jax.ShapeDtypeStruct((rows, cols), jnp.float32)],
        cost_estimate=pl.CostEstimate(
            flops=4 * rows * cols, transcendentals=2 * rows * PACK, bytes_accessed=12 * rows * cols
        ),
    )(kept, got)[0]


def merge(kept, got, split, offset=0):
    rows, cols = kept.shape
    count = 2 if split else 1
    shape = jax.ShapeDtypeStruct((rows // count, cols), jnp.float32)
    if split:
        out_specs = [pl.BlockSpec((rows // 2, cols), lambda i: (0, 0))] * 2
    else:
        out_specs = [pl.BlockSpec((rows, cols), lambda i: (0, 0))]
    return pl.pallas_call(
        merge_kernel,
        grid=(1,),
        in_specs=[
            pl.BlockSpec((rows, cols), lambda i: (0, 0)),
            pl.BlockSpec((rows, cols), lambda i: (offset // rows, 0)),
        ],
        out_specs=out_specs,
        out_shape=[shape] * count,
        cost_estimate=pl.CostEstimate(
            flops=4 * rows * cols, transcendentals=2 * rows * PACK, bytes_accessed=12 * rows * cols
        ),
    )(kept, got)


def finish_kernel(a_ref, b_ref, w_ref, out_ref):
    tmp = a_ref.shape
    merge_kernel(a_ref, b_ref, _Sink(tmp))
    merged = _Sink.value
    width = tmp[1] - PACK
    stats = merged[:, width:]
    stat_lane = lax.broadcasted_iota(jnp.int32, (1, PACK), 1)
    totals = [
        jnp.sum(jnp.where(stat_lane == HEADS + h, stats, 0.0), axis=1, keepdims=True)
        for h in range(HEADS)
    ]
    lane = lax.broadcasted_iota(jnp.int32, (1, 2 * HD), 1)
    low = lane < HD
    blocks = []
    for pair in range(HEADS // 2):
        block = merged[:, pair * 2 * HD : (pair + 1) * 2 * HD]
        blocks.append(block / jnp.where(low, totals[2 * pair], totals[2 * pair + 1]))
    attended = jnp.concatenate(blocks, axis=1)
    square = jnp.mean(attended * attended, axis=1, keepdims=True)
    normed = (attended * lax.rsqrt(square + 1e-06)).astype(jnp.bfloat16)
    out_ref[...] = jnp.dot(normed, w_ref[...], preferred_element_type=jnp.float32)


class _Sink:
    value = None

    def __init__(self, shape):
        self.shape = shape

    def __setitem__(self, index, value):
        _Sink.value = value


def finish(kept, got, w_out):
    rows, cols = kept.shape
    width = w_out.shape[1]
    return pl.pallas_call(
        finish_kernel,
        out_shape=jax.ShapeDtypeStruct((rows, width), jnp.float32),
        cost_estimate=pl.CostEstimate(
            flops=2 * rows * cols * width, transcendentals=rows, bytes_accessed=2 * cols * width
        ),
    )(kept, got, w_out)


def step_bits(nbits, core):
    if nbits != 5:
        return [jnp.int32(b) for b in range(nbits)]
    first, second = [0, 1, 3, 2, 4], [0, 3, 1, 4, 2]
    return [jnp.where(core == 0, a, b) for a, b in zip(first, second)]


def step_pairs(nbits, step):
    pairs = []
    for t in range(1 << nbits):
        bits = [0, 1, 3, 2, 4] if t % 2 == 0 else [0, 3, 1, 4, 2]
        bit = bits[step] if nbits == 5 else step
        pairs.append((t, t ^ (1 << bit)))
    return pairs


def block_order(groups, me):
    nbits = groups.bit_length() - 1
    order = step_bits(nbits, me & 1)
    pos = jnp.arange(groups, dtype=jnp.int32)
    block = jnp.zeros_like(pos)
    for i, bit in enumerate(order):
        a = (pos >> (nbits - 1 - i)) & 1
        block = block + ((a ^ ((me >> bit) & 1)) << bit)
    return block


def tree_reduce(query_rows, hood, listed, keep, w_out):
    groups = lax.axis_size("tm")
    nbits = groups.bit_length() - 1
    qtok = query_rows.shape[0]
    half, quarter = qtok // 2, qtok // 4
    second = attention(query_rows[half:], hood, listed, keep)
    got_first = lax.ppermute(second, "tm", step_pairs(nbits, 0))
    sent = attention(query_rows[quarter:half], hood, listed, keep)
    (sent,) = merge(sent, got_first, False, quarter)
    second = lax.ppermute(sent, "tm", step_pairs(nbits, 1))
    first = attention(query_rows[:quarter], hood, listed, keep)
    (first,) = merge(first, got_first, False, 0)
    for i in range(1, nbits):
        if i == nbits - 1:
            return finish(first, second, w_out)
        rows = first.shape[0] // 2
        sent = merge_part(first, second, rows, rows)
        first = merge_part(first, second, 0, rows)
        second = lax.ppermute(sent, "tm", step_pairs(nbits, i + 1))


def local(queries, kv_blocks, block_list, block_valid, w_out):
    hood = neighbourhood(kv_blocks)
    frames = hood.shape[1]
    nblk = hood.shape[4]
    blk = hood.shape[5]
    width = hood.shape[6]
    hood = hood.reshape(2, frames, 9 * nblk, blk, width)
    listed = block_list[0, 0]
    nlist = listed.shape[0]
    keep = jnp.broadcast_to((block_valid[0, 0] > 0)[:, None, None], (nlist, frames, blk))
    keep = keep.reshape(1, -1).astype(jnp.int32)
    query_rows = queries[0, 0]
    qtok = query_rows.shape[0]
    groups = lax.axis_size("tm")
    me = lax.axis_index("tm")
    order = jnp.concatenate(
        [block_order(groups, me)[: groups // 2], block_order(groups, me ^ 1)[: groups // 2]]
    )
    query_rows = jnp.take(query_rows.reshape(groups, qtok // groups, width), order, axis=0)
    query_rows = query_rows.reshape(qtok, width)
    joined = tree_reduce(query_rows, hood, listed, keep, w_out)
    return joined.reshape(1, 1, joined.shape[0], width)


def solution(mesh):
    in_specs = (
        P("height", "width", None, None),
        P(None, "tm", "height", "width", None, None, None),
        P("height", "width", None),
        P("height", "width", None),
        P(),
    )
    out_specs = P("height", "width", "tm", None)
    return jax.shard_map(local, mesh=mesh, in_specs=in_specs, out_specs=out_specs, check_vma=False)
```
